128 devices in a mesh: dp: 8 (over z, core), expert: 16 (over y, x).
Axes of the slice: x: 4, y: 4, z: 4, core: 2. Of those that a mesh axis runs over, the one named last changes fastest.
Arguments:
- hidden_in: bfloat16 [16384, 2048], P(('dp', 'expert')), may hold values from -40 to 40, as said below
- norm_gain: float32 [2048], replicated, may hold values from 0.5 to 1.5
- router_weight: bfloat16 [2048, 128], replicated, may hold values from -2 to 2, as said below
- grad_out: bfloat16 [16384, 2048], P(('dp', 'expert')), may hold values from -20 to 20, as said below
- expert_ids: int32 [16384, 8], P(('dp', 'expert')), may hold values from 0 to 127, all different within a row; in each aligned block of 128 rows (0 to 127, 128 to 255, ...) at most 9 rows name the same one
- gate_weight: bfloat16 [128, 2048, 768], P(('dp', 'expert')), may hold values from -0.125 to 0.125
- up_weight: bfloat16 [128, 2048, 768], P(('dp', 'expert')), may hold values from -0.125 to 0.125
- down_weight: bfloat16 [128, 768, 2048], P(('dp', 'expert')), may hold values from -0.21875 to 0.21875
Outputs:
- grad_hidden: bfloat16 [16384, 2048], P(('dp', 'expert'))
- grad_router: float32 [2048, 128], replicated
- grad_gain: float32 [2048], replicated
- grad_gate_weight: bfloat16 [128, 2048, 768], P(('dp', 'expert'))
- grad_up_weight: bfloat16 [128, 2048, 768], P(('dp', 'expert'))
- grad_down_weight: bfloat16 [128, 768, 2048], P(('dp', 'expert'))
The draws below stay inside these ranges and needn't reach their ends.
Inputs may be any that keep to these rules, and one draw needn't show every extreme that they name: `expert_ids`: each row names 8 different experts. Among the 128 rows of one device no expert is named more than 9 times; in some devices' rows an expert is named exactly 9 times. `hidden_in`: real values. `router_weight`: real values. `grad_out`: real values.
All inputs are finite; a program needn't handle non-finite values.
Results may differ from the reference program's by a relative error of at most 0.0079.
Values may be sent and summed in bfloat16 or wider, within the bound.
No kernel may reach another device: no remote copies, remote signals or barrier semaphores. Data moves between devices by JAX's collectives and lax.ppermute only.
A program may use at most 128 MiB of HBM per device.

```python
import math
import jax
import jax.numpy as jnp
import numpy as np
from jax import lax

D = 2048
FF = 768
TOPK = 8
TOK_DEV = 128
EXPERTS = 128
CAP = 9
TOKENS = 16384


def draw_hidden_in(key, part):
    noise_part = jax.random.normal(jax.random.fold_in(key, 21), (TOKENS, D), jnp.float32)
    return noise_part.astype(jnp.bfloat16)


def draw_router_weight(key, part):
    noise_part = jax.random.normal(jax.random.fold_in(key, 31), (D, EXPERTS), jnp.float32) * (1.0 / jnp.sqrt(1.0 * D))
    return jnp.clip(noise_part, -2.0, 2.0).astype(jnp.bfloat16)


def draw_grad_out(key, part):
    position = jnp.arange(TOKENS, dtype=jnp.float32)[:, None] / TOKENS
    base_part = jax.random.normal(jax.random.fold_in(key, 43), (TOKENS, D), jnp.float32)
    row_scale = 0.5 + position
    return (base_part * row_scale).astype(jnp.bfloat16)


def block_scale(stream_key, shape, split, low, high):
    level, own = 1.0, jax.random.fold_in(stream_key, 6)
    for dim, parts in split:
        draws = jnp.exp(jax.random.uniform(jax.random.fold_in(own, dim), (parts,), jnp.float32, low / len(split), high / len(split)))
        level = level * jnp.repeat(draws, shape[dim] // parts).reshape([-1 if axis == dim else 1 for axis in range(len(shape))])
    return level


def assign_block(key, own, number, rows, amount, top, limit, slope):
    order = jax.random.permutation(key, amount)
    packed, usual = load_shares(amount, rows * top, limit, slope, True), load_shares(amount, rows * top, limit, slope, False)
    places = jnp.arange(amount)

    def named(tallies, turn):
        used = int((tallies > 0).sum())
        fixed = max(1, used // 4)
        moved = fixed + (places - fixed + turn * (used - fixed)) % max(1, amount - fixed)
        return jnp.zeros((amount,), jnp.int32).at[order[jnp.where(places < fixed, places, moved)]].set(jnp.asarray(tallies, jnp.int32))

    tallies = jnp.where(number % 4 == 0, named(packed, number // 4), named(usual, number - number // 4 - 1))
    mixed = jax.random.permutation(jax.random.fold_in(own, 3), amount)
    giver, taker = mixed[0:amount // 2 * 2:2], mixed[1:amount // 2 * 2:2]
    margin = jnp.minimum(tallies[giver] - 1, limit - tallies[taker]) // 2
    margin = jnp.where((giver == order[0]) | (taker == order[0]) | (tallies[taker] == 0), 0, jnp.maximum(margin, 0))
    moved = jax.random.randint(jax.random.fold_in(own, 4), (amount // 2,), 0, 1 << 20) % (margin + 1)
    tallies = tallies.at[giver].add(-moved).at[taker].add(moved)
    members = jnp.searchsorted(jnp.cumsum(tallies), jnp.arange(rows * top), side="right").astype(jnp.int32)
    grid = members.reshape(top, rows).T
    grid = grid[jax.random.permutation(jax.random.fold_in(own, 1), rows)]
    turn = jax.random.randint(jax.random.fold_in(own, 2), (rows, 1), 0, top)
    return jnp.take_along_axis(grid, (jnp.arange(top)[None, :] + turn) % top, axis=1)


def load_shares(amount, total, bound, slope, full):
    portions = [(1 << 20) // math.isqrt(grade ** slope) + 1 for grade in range(1, amount + 1)]
    largest = bound if full else min(bound, max(-(-total // amount), total * portions[0] // sum(portions)))
    least = 1 if total - largest >= amount - 1 else 0
    given, surplus = [largest] + [least] * (amount - 1), total - largest - least * (amount - 1)
    while surplus > 0:
        movable = [i for i in range(1, amount) if given[i] < largest] or [i for i in range(1, amount) if given[i] < bound]
        whole, budget = sum([portions[i] for i in movable]), surplus
        for i in movable:
            more = min(bound - given[i], max(1, budget * portions[i] // whole), surplus)
            given[i] = given[i] + more
            surplus = surplus - more
    return np.array(given)


def noise(stream_key, shape, deviation, most, split=(), kind=jnp.bfloat16):
    array = deviation * jax.random.normal(stream_key, shape, jnp.float32)
    if split:
        array = array * block_scale(stream_key, shape, split, -0.22, 0.18)
    return jnp.clip(array, -most, most).astype(kind)


def setup_inputs(seed: int = 0) -> dict:
    key_of = jax.random.split(jax.random.key(seed), 9)
    hidden_in = draw_hidden_in(jax.random.fold_in(key_of[8], 71), 0)
    norm_gain = jnp.clip(1.0 + 0.1 * jax.random.normal(key_of[1], (D,), jnp.float32), 0.5, 1.5)
    router_weight = draw_router_weight(jax.random.fold_in(key_of[8], 71), 0)
    grad_out = draw_grad_out(jax.random.fold_in(key_of[8], 71), 0)
    expert_ids_keys = jax.random.split(jax.random.fold_in(key_of[4], 1), TOKENS // TOK_DEV)
    expert_ids_turns = jax.random.permutation(jax.random.fold_in(key_of[4], 3), TOKENS // TOK_DEV)
    expert_ids = jax.vmap(lambda own, number: assign_block(jax.random.fold_in(key_of[4], 2), own, number, TOK_DEV, EXPERTS, TOPK, CAP, 2))(expert_ids_keys, expert_ids_turns).reshape((TOKENS, TOPK))
    gate_weight = noise(key_of[5], (EXPERTS, D, FF), D ** -0.5, 0.125, ((0, 128),))
    up_weight = noise(key_of[6], (EXPERTS, D, FF), D ** -0.5, 0.125, ((0, 128),))
    down_weight = noise(key_of[7], (EXPERTS, FF, D), FF ** -0.5, 0.21875, ((0, 128),))
    return {"hidden_in": hidden_in, "norm_gain": norm_gain, "router_weight": router_weight, "grad_out": grad_out, "expert_ids": expert_ids, "gate_weight": gate_weight, "up_weight": up_weight, "down_weight": down_weight}


def silu_parts(value):
    sigmoid_v = jax.nn.sigmoid(value)
    return (value * sigmoid_v, sigmoid_v * (1.0 + value * (1.0 - sigmoid_v)))

def contract(left, right, left_dim, right_dim):
    return lax.dot_general(left, right, (((left_dim,), (right_dim,)), ((), ())), preferred_element_type=jnp.float32)

def expert_backward(inputs, upstream, prob_rows, gate_mat, up_mat, down_mat):
    pre_gate = jnp.dot(inputs, gate_mat, preferred_element_type=jnp.float32)
    pre_up = jnp.dot(inputs, up_mat, preferred_element_type=jnp.float32)
    activated, derivative = silu_parts(pre_gate)
    hidden_act = activated * pre_up
    grad_mid = contract(upstream, down_mat, 1, 1)
    route_grad = lax.optimization_barrier(jnp.sum(grad_mid * hidden_act, axis=1)).astype(jnp.bfloat16)
    prob_col = prob_rows.astype(jnp.float32)[:, None]
    scaled = prob_col * grad_mid
    grad_pre_gate = (scaled * pre_up * derivative).astype(jnp.bfloat16)
    grad_pre_up = (scaled * activated).astype(jnp.bfloat16)
    scaled_up = (prob_col * upstream.astype(jnp.float32)).astype(jnp.bfloat16)
    grad_gate_mat = contract(inputs, grad_pre_gate, 0, 0).astype(jnp.bfloat16)
    grad_up_mat = contract(inputs, grad_pre_up, 0, 0).astype(jnp.bfloat16)
    grad_down_mat = contract(hidden_act.astype(jnp.bfloat16), scaled_up, 0, 0).astype(jnp.bfloat16)
    grad_inputs = (contract(grad_pre_gate, gate_mat, 1, 1) + contract(grad_pre_up, up_mat, 1, 1)).astype(jnp.bfloat16)
    return (grad_gate_mat, grad_up_mat, grad_down_mat, grad_inputs, route_grad)

def block_slots(block_ids):
    onehot = (block_ids[:, None] == jnp.arange(EXPERTS, dtype=jnp.int32)[None, :]).astype(jnp.int32)
    counts = jnp.cumsum(onehot, axis=0)
    return (lax.optimization_barrier(jnp.sum(counts * onehot, axis=1)) - 1).astype(jnp.int32)

def reference(hidden_in, norm_gain, router_weight, grad_out, expert_ids, gate_weight, up_weight, down_weight):
    values = hidden_in.astype(jnp.float32)
    inv_rms = lax.rsqrt(lax.optimization_barrier(jnp.mean(values * values, axis=1, keepdims=True)) + 1e-06)
    normed = (values * inv_rms * norm_gain).astype(jnp.bfloat16)
    logits = jnp.dot(normed, router_weight, preferred_element_type=jnp.float32)
    picked = jnp.take_along_axis(logits, expert_ids, axis=1)
    route_prob = jax.nn.softmax(picked, axis=1)
    prob_bf = route_prob.astype(jnp.bfloat16)
    blocks = TOKENS // TOK_DEV
    routes = TOK_DEV * TOPK
    total_routes = TOKENS * TOPK
    block_ids = expert_ids.reshape(blocks, routes)
    slot_idx = lax.map(block_slots, block_ids)
    block_col = jnp.arange(blocks, dtype=jnp.int32)[:, None]
    target = ((block_ids * blocks + block_col) * CAP + slot_idx).astype(jnp.int32)
    flat_target = target.reshape(-1)
    owner_idx = jnp.full((EXPERTS * blocks * CAP,), total_routes, jnp.int32).at[flat_target].set(jnp.arange(total_routes, dtype=jnp.int32))
    token_of = jnp.where(owner_idx < total_routes, owner_idx // TOPK, TOKENS).astype(jnp.int32).reshape(EXPERTS, blocks * CAP)
    owner_rows = owner_idx.reshape(EXPERTS, blocks * CAP)
    pad_normed = jnp.concatenate([normed, jnp.zeros((1, D), jnp.bfloat16)], axis=0)
    pad_grads = jnp.concatenate([grad_out, jnp.zeros((1, D), jnp.bfloat16)], axis=0)
    pad_probs = jnp.concatenate([prob_bf.reshape(-1), jnp.zeros((1,), jnp.bfloat16)], axis=0)

    def per_expert(expert_items):
        token_rows, owners, gate_mat, up_mat, down_mat = expert_items
        return expert_backward(pad_normed[token_rows], pad_grads[token_rows], pad_probs[owners], gate_mat, up_mat, down_mat)
    grad_gate_weight, grad_up_weight, grad_down_weight, slot_input, slot_grad = lax.map(per_expert, (token_of, owner_rows, gate_weight, up_weight, down_weight))
    input_flat = slot_input.reshape(-1, D)
    target_tk = flat_target.reshape(TOKENS, TOPK)
    route_sum = jnp.zeros((TOKENS, D), jnp.float32)
    for position in range(TOPK):
        route_sum = route_sum + input_flat[target_tk[:, position]].astype(jnp.float32)
    grad_prob = slot_grad.reshape(-1)[target_tk].astype(jnp.float32)
    grad_picked = route_prob * (grad_prob - lax.optimization_barrier(jnp.sum(route_prob * grad_prob, axis=1, keepdims=True)))
    token_idx = jnp.broadcast_to(jnp.arange(TOKENS, dtype=jnp.int32)[:, None], (TOKENS, TOPK))
    grad_logit = jnp.zeros((TOKENS, EXPERTS), jnp.float32).at[token_idx, expert_ids].add(grad_picked).astype(jnp.bfloat16)
    grad_router = contract(normed, grad_logit, 0, 0)
    grad_normed = route_sum + contract(grad_logit, router_weight, 1, 1)
    grad_gain = lax.optimization_barrier(jnp.sum(grad_normed * values * inv_rms, axis=0))
    scaled = norm_gain * grad_normed
    cube = inv_rms * inv_rms * inv_rms
    grad_hidden = (grad_out.astype(jnp.float32) + inv_rms * scaled - values * cube * lax.optimization_barrier(jnp.mean(scaled * values, axis=1, keepdims=True))).astype(jnp.bfloat16)
    return (grad_hidden, grad_router, grad_gain, grad_gate_weight, grad_up_weight, grad_down_weight)
```

```python
import jax
import jax.numpy as jnp
from jax import lax
from jax.sharding import PartitionSpec as P


def silu_parts(value):
    sigmoid_v = jax.nn.sigmoid(value)
    return (value * sigmoid_v, sigmoid_v * (1.0 + value * (1.0 - sigmoid_v)))


def dims(left, right, left_dims, right_dims):
    return lax.dot_general(
        left, right, ((left_dims, right_dims), ((), ())), preferred_element_type=jnp.float32
    )


def expert_backward(rows_x, rows_y, prob_rows, gate_mat, up_mat, down_mat):
    slots, chunks, lanes = rows_x.shape
    ff = gate_mat.shape[1]
    gate3 = gate_mat.reshape(chunks, lanes, ff)
    up3 = up_mat.reshape(chunks, lanes, ff)
    down3 = down_mat.reshape(ff, chunks, lanes)
    pre_gate = dims(rows_x, gate3, (1, 2), (0, 1))
    pre_up = dims(rows_x, up3, (1, 2), (0, 1))
    activated, derivative = silu_parts(pre_gate)
    hidden_act = activated * pre_up
    grad_mid = dims(rows_y, down3, (1, 2), (1, 2))
    route_grad = jnp.sum(grad_mid * hidden_act, axis=1).astype(jnp.bfloat16)
    prob_col = prob_rows.astype(jnp.float32)[:, None]
    scaled = prob_col * grad_mid
    grad_pre_gate = (scaled * pre_up * derivative).astype(jnp.bfloat16)
    grad_pre_up = (scaled * activated).astype(jnp.bfloat16)
    scaled_up = (prob_col[:, :, None] * rows_y.astype(jnp.float32)).astype(jnp.bfloat16)
    grad_gate_mat = dims(rows_x, grad_pre_gate, (0,), (0,)).astype(jnp.bfloat16)
    grad_up_mat = dims(rows_x, grad_pre_up, (0,), (0,)).astype(jnp.bfloat16)
    grad_down_mat = dims(hidden_act.astype(jnp.bfloat16), scaled_up, (0,), (0,)).astype(jnp.bfloat16)
    grad_inputs = (
        dims(grad_pre_gate, gate3, (1,), (2,)) + dims(grad_pre_up, up3, (1,), (2,))
    ).astype(jnp.bfloat16)
    return (
        grad_gate_mat.reshape(chunks * lanes, ff),
        grad_up_mat.reshape(chunks * lanes, ff),
        grad_down_mat.reshape(ff, chunks * lanes),
        grad_inputs,
        route_grad,
    )


def local(
    hidden_in, norm_gain, router_weight, grad_out, expert_ids, gate_weight, up_weight, down_weight
):
    f32, bf16 = jnp.float32, jnp.bfloat16
    tok_rows, model_width = hidden_in.shape
    top_count = expert_ids.shape[1]
    experts = router_weight.shape[1]
    capacity = max(2, (tok_rows * top_count * 9 + 8 * experts - 1) // (8 * experts))
    slots = experts * capacity
    lanes = 128
    chunks = model_width // lanes
    axes = ("dp", "expert")

    values = hidden_in.astype(f32)
    inv_rms = lax.rsqrt(jnp.mean(values * values, axis=1, keepdims=True) + 1e-06)
    normed = (values * inv_rms * norm_gain).astype(bf16)
    logits = jnp.dot(normed, router_weight, preferred_element_type=f32)
    chosen = expert_ids[:, :, None] == jnp.arange(experts, dtype=jnp.int32)[None, None, :]
    picked = jnp.sum(jnp.where(chosen, logits[:, None, :], 0.0), axis=2)
    route_prob = jax.nn.softmax(picked, axis=1)
    prob_bf = route_prob.astype(bf16)

    flat_ids = expert_ids.reshape(-1)
    onehot = (flat_ids[:, None] == jnp.arange(experts, dtype=jnp.int32)[None, :]).astype(jnp.int32)
    counts = jnp.cumsum(onehot, axis=0)
    slot_idx = jnp.sum(counts * onehot, axis=1) - 1
    target = (flat_ids * capacity + slot_idx).reshape(tok_rows, top_count)
    hit = target[None, :, :] == jnp.arange(slots, dtype=jnp.int32)[:, None, None]
    sel_tok = jnp.any(hit, axis=2).astype(bf16)
    send_p = jnp.sum(jnp.where(hit, prob_bf.astype(f32)[None], 0.0), axis=(1, 2)).astype(bf16)

    normed3 = normed.reshape(tok_rows, chunks, lanes)
    grads3 = grad_out.reshape(tok_rows, chunks, lanes)
    send_x = dims(sel_tok, normed3, (1,), (0,)).astype(bf16).reshape(experts, capacity, chunks, lanes)
    send_y = dims(sel_tok, grads3, (1,), (0,)).astype(bf16).reshape(experts, capacity, chunks, lanes)
    recv_x = lax.all_to_all(send_x, axes, 0, 0, tiled=True)
    recv_y = lax.all_to_all(send_y, axes, 0, 0, tiled=True)
    recv_p = lax.all_to_all(send_p.reshape(experts, capacity), axes, 0, 0, tiled=True)

    grad_gate_mat, grad_up_mat, grad_down_mat, grad_inputs, route_grad = expert_backward(
        recv_x.reshape(slots, chunks, lanes),
        recv_y.reshape(slots, chunks, lanes),
        recv_p.reshape(slots),
        gate_weight[0],
        up_weight[0],
        down_weight[0],
    )
    back_inputs = lax.all_to_all(
        grad_inputs.reshape(experts, capacity, chunks, lanes), axes, 0, 0, tiled=True
    )
    back_grads = lax.all_to_all(route_grad.reshape(experts, capacity), axes, 0, 0, tiled=True)

    route_sum = dims(sel_tok, back_inputs.reshape(slots, chunks, lanes), (0,), (0,)).reshape(
        tok_rows, model_width
    )
    grad_prob = jnp.sum(
        jnp.where(hit, back_grads.reshape(slots).astype(f32)[:, None, None], 0.0), axis=0
    )
    grad_picked = route_prob * (grad_prob - jnp.sum(route_prob * grad_prob, axis=1, keepdims=True))
    grad_logit = jnp.sum(jnp.where(chosen, grad_picked[:, :, None], 0.0), axis=1).astype(bf16)
    router_part = dims(normed, grad_logit, (0,), (0,))
    grad_normed = route_sum + dims(grad_logit, router_weight, (1,), (1,))
    gain_part = jnp.sum(grad_normed * values * inv_rms, axis=0)
    packed = jnp.concatenate([router_part, gain_part.reshape(-1, experts)], axis=0)
    packed = lax.psum(packed, axes)
    grad_router = packed[:model_width]
    grad_gain = packed[model_width:].reshape(model_width)
    scaled = norm_gain * grad_normed
    cube = inv_rms * inv_rms * inv_rms
    grad_hidden = (
        grad_out.astype(f32)
        + inv_rms * scaled
        - values * cube * jnp.mean(scaled * values, axis=1, keepdims=True)
    ).astype(bf16)
    return (
        grad_hidden,
        grad_router,
        grad_gain,
        grad_gate_mat[None],
        grad_up_mat[None],
        grad_down_mat[None],
    )


def solution(mesh):
    in_specs = (
        P(("dp", "expert"), None),
        P(),
        P(),
        P(("dp", "expert"), None),
        P(("dp", "expert"), None),
        P(("dp", "expert"), None, None),
        P(("dp", "expert"), None, None),
        P(("dp", "expert"), None, None),
    )
    out_specs = (
        P(("dp", "expert"), None),
        P(),
        P(),
        P(("dp", "expert"), None, None),
        P(("dp", "expert"), None, None),
        P(("dp", "expert"), None, None),
    )
    return jax.shard_map(local, mesh=mesh, in_specs=in_specs, out_specs=out_specs, check_vma=False)
```

```python
import jax
import jax.numpy as jnp
from jax import lax
from jax.sharding import PartitionSpec as P


def silu_parts(value):
    sigmoid_v = jax.nn.sigmoid(value)
    return (value * sigmoid_v, sigmoid_v * (1.0 + value * (1.0 - sigmoid_v)))


def dims(left, right, left_dims, right_dims):
    return lax.dot_general(
        left, right, ((left_dims, right_dims), ((), ())), preferred_element_type=jnp.float32
    )


def expert_backward(rows_x, rows_y, prob_rows, gate_mat, up_mat, down_mat):
    slots, chunks, lanes = rows_x.shape
    ff = gate_mat.shape[1]
    gate3 = gate_mat.reshape(chunks, lanes, ff)
    up3 = up_mat.reshape(chunks, lanes, ff)
    down3 = down_mat.reshape(ff, chunks, lanes)
    pre_gate = dims(rows_x, gate3, (1, 2), (0, 1))
    pre_up = dims(rows_x, up3, (1, 2), (0, 1))
    activated, derivative = silu_parts(pre_gate)
    hidden_act = activated * pre_up
    grad_mid = dims(rows_y, down3, (1, 2), (1, 2))
    route_grad = jnp.sum(grad_mid * hidden_act, axis=1).astype(jnp.bfloat16)
    prob_col = prob_rows.astype(jnp.float32)[:, None]
    scaled = prob_col * grad_mid
    grad_pre_gate = (scaled * pre_up * derivative).astype(jnp.bfloat16)
    grad_pre_up = (scaled * activated).astype(jnp.bfloat16)
    scaled_up = (prob_col[:, :, None] * rows_y.astype(jnp.float32)).astype(jnp.bfloat16)
    grad_gate_mat = dims(rows_x, grad_pre_gate, (0,), (0,)).astype(jnp.bfloat16)
    grad_up_mat = dims(rows_x, grad_pre_up, (0,), (0,)).astype(jnp.bfloat16)
    grad_down_mat = dims(hidden_act.astype(jnp.bfloat16), scaled_up, (0,), (0,)).astype(jnp.bfloat16)
    grad_inputs = (
        dims(grad_pre_gate, gate3, (1,), (2,)) + dims(grad_pre_up, up3, (1,), (2,))
    ).astype(jnp.bfloat16)
    return (
        grad_gate_mat.reshape(chunks * lanes, ff),
        grad_up_mat.reshape(chunks * lanes, ff),
        grad_down_mat.reshape(ff, chunks * lanes),
        grad_inputs,
        route_grad,
    )


def local(
    hidden_in, norm_gain, router_weight, grad_out, expert_ids, gate_weight, up_weight, down_weight
):
    f32, bf16 = jnp.float32, jnp.bfloat16
    tok_rows, model_width = hidden_in.shape
    top_count = expert_ids.shape[1]
    experts = router_weight.shape[1]
    capacity = max(2, (tok_rows * top_count * 9 + 8 * experts - 1) // (8 * experts))
    slots = experts * capacity
    lanes = 128
    chunks = model_width // lanes
    axes = ("dp", "expert")

    values = hidden_in.astype(f32)
    inv_rms = lax.rsqrt(jnp.mean(values * values, axis=1, keepdims=True) + 1e-06)
    normed = (values * inv_rms * norm_gain).astype(bf16)
    logits = jnp.dot(normed, router_weight, preferred_element_type=f32)
    chosen = expert_ids[:, :, None] == jnp.arange(experts, dtype=jnp.int32)[None, None, :]
    picked = jnp.sum(jnp.where(chosen, logits[:, None, :], 0.0), axis=2)
    route_prob = jax.nn.softmax(picked, axis=1)
    prob_bf = route_prob.astype(bf16)

    flat_ids = expert_ids.reshape(-1)
    onehot = (flat_ids[:, None] == jnp.arange(experts, dtype=jnp.int32)[None, :]).astype(jnp.int32)
    counts = jnp.cumsum(onehot, axis=0)
    slot_idx = jnp.sum(counts * onehot, axis=1) - 1
    target = (flat_ids * capacity + slot_idx).reshape(tok_rows, top_count)
    hit = target[None, :, :] == jnp.arange(slots, dtype=jnp.int32)[:, None, None]
    sel_tok = jnp.any(hit, axis=2).astype(bf16)
    send_p = jnp.sum(jnp.where(hit, prob_bf.astype(f32)[None], 0.0), axis=(1, 2)).astype(bf16)

    normed3 = normed.reshape(tok_rows, chunks, lanes)
    grads3 = grad_out.reshape(tok_rows, chunks, lanes)
    send_x = dims(sel_tok, normed3, (1,), (0,)).astype(bf16).reshape(experts, capacity, chunks, lanes)
    send_y = dims(sel_tok, grads3, (1,), (0,)).astype(bf16).reshape(experts, capacity, chunks, lanes)
    recv_x = lax.all_to_all(send_x, axes, 0, 0, tiled=True)
    recv_y = lax.all_to_all(send_y, axes, 0, 0, tiled=True)
    recv_p = lax.all_to_all(send_p.reshape(experts, capacity), axes, 0, 0, tiled=True)

    grad_gate_mat, grad_up_mat, grad_down_mat, grad_inputs, route_grad = expert_backward(
        recv_x.reshape(slots, chunks, lanes),
        recv_y.reshape(slots, chunks, lanes),
        recv_p.reshape(slots),
        gate_weight[0],
        up_weight[0],
        down_weight[0],
    )
    back_inputs = lax.all_to_all(
        grad_inputs.reshape(experts, capacity, chunks, lanes), axes, 0, 0, tiled=True
    )
    back_grads = lax.all_to_all(route_grad.reshape(experts, capacity), axes, 0, 0, tiled=True)

    route_sum = dims(sel_tok, back_inputs.reshape(slots, chunks, lanes), (0,), (0,)).reshape(
        tok_rows, model_width
    )
    grad_prob = back_grads.reshape(slots)[target].astype(f32)
    grad_picked = route_prob * (grad_prob - jnp.sum(route_prob * grad_prob, axis=1, keepdims=True))
    grad_logit = jnp.sum(jnp.where(chosen, grad_picked[:, :, None], 0.0), axis=1).astype(bf16)
    router_part = dims(normed, grad_logit, (0,), (0,))
    grad_normed = route_sum + dims(grad_logit, router_weight, (1,), (1,))
    gain_part = jnp.sum(grad_normed * values * inv_rms, axis=0)
    n_dev = experts
    rows_per = model_width // n_dev
    gain_per = model_width // n_dev
    gain_rows = jnp.pad(gain_part.reshape(n_dev, 1, gain_per), ((0, 0), (0, 0), (0, experts - gain_per)))
    send_sum = jnp.concatenate([router_part.reshape(n_dev, rows_per, experts), gain_rows], axis=1)
    part_sum = jnp.sum(lax.all_to_all(send_sum, axes, 0, 0, tiled=True), axis=0)
    whole = lax.all_to_all(
        jnp.broadcast_to(part_sum[None], (n_dev,) + part_sum.shape), axes, 0, 0, tiled=True
    )
    grad_router = whole[:, :rows_per, :].reshape(model_width, experts)
    grad_gain = whole[:, rows_per, :gain_per].reshape(model_width)
    scaled = norm_gain * grad_normed
    cube = inv_rms * inv_rms * inv_rms
    grad_hidden = (
        grad_out.astype(f32)
        + inv_rms * scaled
        - values * cube * jnp.mean(scaled * values, axis=1, keepdims=True)
    ).astype(bf16)
    return (
        grad_hidden,
        grad_router,
        grad_gain,
        grad_gate_mat[None],
        grad_up_mat[None],
        grad_down_mat[None],
    )


def solution(mesh):
    in_specs = (
        P(("dp", "expert"), None),
        P(),
        P(),
        P(("dp", "expert"), None),
        P(("dp", "expert"), None),
        P(("dp", "expert"), None, None),
        P(("dp", "expert"), None, None),
        P(("dp", "expert"), None, None),
    )
    out_specs = (
        P(("dp", "expert"), None),
        P(),
        P(),
        P(("dp", "expert"), None, None),
        P(("dp", "expert"), None, None),
        P(("dp", "expert"), None, None),
    )
    return jax.shard_map(local, mesh=mesh, in_specs=in_specs, out_specs=out_specs, check_vma=False)
```

```python
import jax
import jax.numpy as jnp
from jax import lax
from jax.sharding import PartitionSpec as P


def silu_parts(value):
    sigmoid_v = jax.nn.sigmoid(value)
    return (value * sigmoid_v, sigmoid_v * (1.0 + value * (1.0 - sigmoid_v)))


def dims(left, right, left_dims, right_dims):
    return lax.dot_general(
        left, right, ((left_dims, right_dims), ((), ())), preferred_element_type=jnp.float32
    )


def expert_backward(rows_x, rows_y, prob_rows, gate_mat, up_mat, down_mat):
    slots, chunks, lanes = rows_x.shape
    ff = gate_mat.shape[1]
    gate3 = gate_mat.reshape(chunks, lanes, ff)
    up3 = up_mat.reshape(chunks, lanes, ff)
    down3 = down_mat.reshape(ff, chunks, lanes)
    pre_gate = dims(rows_x, gate3, (1, 2), (0, 1))
    pre_up = dims(rows_x, up3, (1, 2), (0, 1))
    activated, derivative = silu_parts(pre_gate)
    hidden_act = activated * pre_up
    grad_mid = dims(rows_y, down3, (1, 2), (1, 2))
    route_grad = jnp.sum(grad_mid * hidden_act, axis=1).astype(jnp.bfloat16)
    prob_col = prob_rows.astype(jnp.float32)[:, None]
    scaled = prob_col * grad_mid
    grad_pre_gate = (scaled * pre_up * derivative).astype(jnp.bfloat16)
    grad_pre_up = (scaled * activated).astype(jnp.bfloat16)
    scaled_up = (prob_col[:, :, None] * rows_y.astype(jnp.float32)).astype(jnp.bfloat16)
    grad_gate_mat = dims(rows_x, grad_pre_gate, (0,), (0,)).astype(jnp.bfloat16)
    grad_up_mat = dims(rows_x, grad_pre_up, (0,), (0,)).astype(jnp.bfloat16)
    grad_down_mat = dims(hidden_act.astype(jnp.bfloat16), scaled_up, (0,), (0,)).astype(jnp.bfloat16)
    grad_inputs = (
        dims(grad_pre_gate, gate3, (1,), (2,)) + dims(grad_pre_up, up3, (1,), (2,))
    ).astype(jnp.bfloat16)
    return (
        grad_gate_mat.reshape(chunks * lanes, ff),
        grad_up_mat.reshape(chunks * lanes, ff),
        grad_down_mat.reshape(ff, chunks * lanes),
        grad_inputs,
        route_grad,
    )


def local(
    hidden_in, norm_gain, router_weight, grad_out, expert_ids, gate_weight, up_weight, down_weight
):
    f32, bf16 = jnp.float32, jnp.bfloat16
    tok_rows, model_width = hidden_in.shape
    top_count = expert_ids.shape[1]
    experts = router_weight.shape[1]
    capacity = max(2, (tok_rows * top_count * 9 + 8 * experts - 1) // (8 * experts))
    slots = experts * capacity
    routes = tok_rows * top_count
    lanes = 128
    chunks = model_width // lanes
    axes = ("dp", "expert")

    values = hidden_in.astype(f32)
    inv_rms = lax.rsqrt(jnp.mean(values * values, axis=1, keepdims=True) + 1e-06)
    normed = (values * inv_rms * norm_gain).astype(bf16)
    logits = jnp.dot(normed, router_weight, preferred_element_type=f32)
    chosen = expert_ids[:, :, None] == jnp.arange(experts, dtype=jnp.int32)[None, None, :]
    picked = jnp.sum(jnp.where(chosen, logits[:, None, :], 0.0), axis=2)
    route_prob = jax.nn.softmax(picked, axis=1)
    prob_bf = route_prob.astype(bf16)

    flat_ids = expert_ids.reshape(-1)
    onehot = (flat_ids[:, None] == jnp.arange(experts, dtype=jnp.int32)[None, :]).astype(jnp.int32)
    counts = jnp.cumsum(onehot, axis=0)
    slot_idx = jnp.sum(counts * onehot, axis=1) - 1
    target = (flat_ids * capacity + slot_idx).reshape(tok_rows, top_count)
    owner = (
        jnp.full((slots,), routes, jnp.int32)
        .at[target.reshape(-1)]
        .set(jnp.arange(routes, dtype=jnp.int32))
    )
    token_of = jnp.minimum(owner // top_count, tok_rows)
    pad_probs = jnp.concatenate([prob_bf.reshape(-1), jnp.zeros((1,), bf16)], axis=0)
    send_p = pad_probs[owner]

    both3 = jnp.concatenate(
        [
            normed.reshape(tok_rows, chunks, lanes),
            grad_out.reshape(tok_rows, chunks, lanes),
        ],
        axis=1,
    )
    both3 = jnp.concatenate([both3, jnp.zeros((1, 2 * chunks, lanes), bf16)], axis=0)
    send_xy = both3[token_of].reshape(experts, capacity, 2 * chunks, lanes)
    recv_xy = lax.all_to_all(send_xy, axes, 0, 0, tiled=True).reshape(slots, 2 * chunks, lanes)
    recv_p = lax.all_to_all(send_p.reshape(experts, capacity), axes, 0, 0, tiled=True)

    grad_gate_mat, grad_up_mat, grad_down_mat, grad_inputs, route_grad = expert_backward(
        recv_xy[:, :chunks],
        recv_xy[:, chunks:],
        recv_p.reshape(slots),
        gate_weight[0],
        up_weight[0],
        down_weight[0],
    )
    back_inputs = lax.all_to_all(
        grad_inputs.reshape(experts, capacity, chunks, lanes), axes, 0, 0, tiled=True
    )
    back_grads = lax.all_to_all(route_grad.reshape(experts, capacity), axes, 0, 0, tiled=True)

    back3 = back_inputs.reshape(slots, chunks, lanes)
    route_sum = jnp.sum(back3[target].astype(f32), axis=1).reshape(tok_rows, model_width)
    grad_prob = back_grads.reshape(slots)[target].astype(f32)
    grad_picked = route_prob * (grad_prob - jnp.sum(route_prob * grad_prob, axis=1, keepdims=True))
    grad_logit = jnp.sum(jnp.where(chosen, grad_picked[:, :, None], 0.0), axis=1).astype(bf16)
    router_part = dims(normed, grad_logit, (0,), (0,))
    grad_normed = route_sum + dims(grad_logit, router_weight, (1,), (1,))
    gain_part = jnp.sum(grad_normed * values * inv_rms, axis=0)
    n_dev = experts
    rows_per = model_width // n_dev
    gain_per = model_width // n_dev
    gain_rows = jnp.pad(gain_part.reshape(n_dev, 1, gain_per), ((0, 0), (0, 0), (0, experts - gain_per)))
    send_sum = jnp.concatenate([router_part.reshape(n_dev, rows_per, experts), gain_rows], axis=1)
    part_sum = jnp.sum(lax.all_to_all(send_sum, axes, 0, 0, tiled=True), axis=0)
    whole = lax.all_to_all(
        jnp.broadcast_to(part_sum[None], (n_dev,) + part_sum.shape), axes, 0, 0, tiled=True
    )
    grad_router = whole[:, :rows_per, :].reshape(model_width, experts)
    grad_gain = whole[:, rows_per, :gain_per].reshape(model_width)
    scaled = norm_gain * grad_normed
    cube = inv_rms * inv_rms * inv_rms
    grad_hidden = (
        grad_out.astype(f32)
        + inv_rms * scaled
        - values * cube * jnp.mean(scaled * values, axis=1, keepdims=True)
    ).astype(bf16)
    return (
        grad_hidden,
        grad_router,
        grad_gain,
        grad_gate_mat[None],
        grad_up_mat[None],
        grad_down_mat[None],
    )


def solution(mesh):
    in_specs = (
        P(("dp", "expert"), None),
        P(),
        P(),
        P(("dp", "expert"), None),
        P(("dp", "expert"), None),
        P(("dp", "expert"), None, None),
        P(("dp", "expert"), None, None),
        P(("dp", "expert"), None, None),
    )
    out_specs = (
        P(("dp", "expert"), None),
        P(),
        P(),
        P(("dp", "expert"), None, None),
        P(("dp", "expert"), None, None),
        P(("dp", "expert"), None, None),
    )
    return jax.shard_map(local, mesh=mesh, in_specs=in_specs, out_specs=out_specs, check_vma=False)
```

```python
import jax
import jax.numpy as jnp
from jax import lax
from jax.sharding import PartitionSpec as P


def silu_parts(value):
    sigmoid_v = jax.nn.sigmoid(value)
    return (value * sigmoid_v, sigmoid_v * (1.0 + value * (1.0 - sigmoid_v)))


def dims(left, right, left_dims, right_dims):
    return lax.dot_general(
        left, right, ((left_dims, right_dims), ((), ())), preferred_element_type=jnp.float32
    )


def expert_backward(rows_x, rows_y, prob_rows, gate_mat, up_mat, down_mat):
    slots, chunks, lanes = rows_x.shape
    ff = gate_mat.shape[1]
    gate3 = gate_mat.reshape(chunks, lanes, ff)
    up3 = up_mat.reshape(chunks, lanes, ff)
    down3 = down_mat.reshape(ff, chunks, lanes)
    pre_gate = dims(rows_x, gate3, (1, 2), (0, 1))
    pre_up = dims(rows_x, up3, (1, 2), (0, 1))
    activated, derivative = silu_parts(pre_gate)
    hidden_act = activated * pre_up
    grad_mid = dims(rows_y, down3, (1, 2), (1, 2))
    route_grad = jnp.sum(grad_mid * hidden_act, axis=1).astype(jnp.bfloat16)
    prob_col = prob_rows.astype(jnp.float32)[:, None]
    scaled = prob_col * grad_mid
    grad_pre_gate = (scaled * pre_up * derivative).astype(jnp.bfloat16)
    grad_pre_up = (scaled * activated).astype(jnp.bfloat16)
    scaled_up = (prob_col[:, :, None] * rows_y.astype(jnp.float32)).astype(jnp.bfloat16)
    grad_gate_mat = dims(rows_x, grad_pre_gate, (0,), (0,))
    grad_up_mat = dims(rows_x, grad_pre_up, (0,), (0,))
    grad_down_mat = dims(hidden_act.astype(jnp.bfloat16), scaled_up, (0,), (0,))
    grad_inputs = (
        dims(grad_pre_gate, gate3, (1,), (2,)) + dims(grad_pre_up, up3, (1,), (2,))
    ).astype(jnp.bfloat16)
    return (
        grad_gate_mat.reshape(chunks * lanes, ff),
        grad_up_mat.reshape(chunks * lanes, ff),
        grad_down_mat.reshape(ff, chunks * lanes),
        grad_inputs,
        route_grad,
    )


def local(
    hidden_in, norm_gain, router_weight, grad_out, expert_ids, gate_weight, up_weight, down_weight
):
    f32, bf16 = jnp.float32, jnp.bfloat16
    tok_rows, model_width = hidden_in.shape
    top_count = expert_ids.shape[1]
    experts = router_weight.shape[1]
    capacity = max(2, (tok_rows * top_count * 9 + 8 * experts - 1) // (8 * experts))
    slots = experts * capacity
    routes = tok_rows * top_count
    lanes = 128
    chunks = model_width // lanes
    axes = ("dp", "expert")

    values = hidden_in.astype(f32)
    inv_rms = lax.rsqrt(jnp.mean(values * values, axis=1, keepdims=True) + 1e-06)
    normed = (values * inv_rms * norm_gain).astype(bf16)
    logits = jnp.dot(normed, router_weight, preferred_element_type=f32)
    chosen = expert_ids[:, :, None] == jnp.arange(experts, dtype=jnp.int32)[None, None, :]
    picked = jnp.sum(jnp.where(chosen, logits[:, None, :], 0.0), axis=2)
    route_prob = jax.nn.softmax(picked, axis=1)
    prob_bf = route_prob.astype(bf16)

    flat_ids = expert_ids.reshape(-1)
    onehot = (flat_ids[:, None] == jnp.arange(experts, dtype=jnp.int32)[None, :]).astype(jnp.int32)
    counts = jnp.cumsum(onehot, axis=0)
    slot_idx = jnp.sum(counts * onehot, axis=1) - 1
    target = (flat_ids * capacity + slot_idx).reshape(tok_rows, top_count)
    owner = (
        jnp.full((slots,), routes, jnp.int32)
        .at[target.reshape(-1)]
        .set(jnp.arange(routes, dtype=jnp.int32))
    )
    token_of = jnp.minimum(owner // top_count, tok_rows)
    pad_probs = jnp.concatenate([prob_bf.reshape(-1), jnp.zeros((1,), bf16)], axis=0)
    send_p = pad_probs[owner]

    both3 = jnp.concatenate(
        [
            normed.reshape(tok_rows, chunks, lanes),
            grad_out.reshape(tok_rows, chunks, lanes),
        ],
        axis=1,
    )
    both3 = jnp.concatenate([both3, jnp.zeros((1, 2 * chunks, lanes), bf16)], axis=0)
    token_grid = token_of.reshape(experts, capacity)
    prob_grid = lax.all_to_all(send_p.reshape(experts, capacity), axes, 0, 0, tiled=True)
    half = (capacity + 1) // 2
    sums, back_parts, grad_parts = None, [], []
    for low, high in ((0, half), (half, capacity)):
        width = high - low
        send_xy = both3[token_grid[:, low:high]]
        recv_xy = lax.all_to_all(send_xy, axes, 0, 0, tiled=True).reshape(
            experts * width, 2 * chunks, lanes
        )
        part = expert_backward(
            recv_xy[:, :chunks],
            recv_xy[:, chunks:],
            prob_grid[:, low:high].reshape(-1),
            gate_weight[0],
            up_weight[0],
            down_weight[0],
        )
        sums = part[:3] if sums is None else tuple(a + b for a, b in zip(sums, part[:3]))
        back_parts.append(
            lax.all_to_all(
                part[3].reshape(experts, width, chunks, lanes), axes, 0, 0, tiled=True
            )
        )
        grad_parts.append(part[4].reshape(experts, width))
    grad_gate_mat, grad_up_mat, grad_down_mat = (a.astype(bf16) for a in sums)
    back_inputs = jnp.concatenate(back_parts, axis=1)
    back_grads = lax.all_to_all(jnp.concatenate(grad_parts, axis=1), axes, 0, 0, tiled=True)

    back3 = back_inputs.reshape(slots, chunks, lanes)
    route_sum = jnp.sum(back3[target].astype(f32), axis=1).reshape(tok_rows, model_width)
    grad_prob = back_grads.reshape(slots)[target].astype(f32)
    grad_picked = route_prob * (grad_prob - jnp.sum(route_prob * grad_prob, axis=1, keepdims=True))
    grad_logit = jnp.sum(jnp.where(chosen, grad_picked[:, :, None], 0.0), axis=1).astype(bf16)
    router_part = dims(normed, grad_logit, (0,), (0,))
    grad_normed = route_sum + dims(grad_logit, router_weight, (1,), (1,))
    gain_part = jnp.sum(grad_normed * values * inv_rms, axis=0)
    n_dev = experts
    rows_per = model_width // n_dev
    gain_per = model_width // n_dev
    gain_rows = jnp.pad(gain_part.reshape(n_dev, 1, gain_per), ((0, 0), (0, 0), (0, experts - gain_per)))
    send_sum = jnp.concatenate([router_part.reshape(n_dev, rows_per, experts), gain_rows], axis=1)
    part_sum = jnp.sum(lax.all_to_all(send_sum, axes, 0, 0, tiled=True), axis=0)
    whole = lax.all_to_all(
        jnp.broadcast_to(part_sum[None], (n_dev,) + part_sum.shape), axes, 0, 0, tiled=True
    )
    grad_router = whole[:, :rows_per, :].reshape(model_width, experts)
    grad_gain = whole[:, rows_per, :gain_per].reshape(model_width)
    scaled = norm_gain * grad_normed
    cube = inv_rms * inv_rms * inv_rms
    grad_hidden = (
        grad_out.astype(f32)
        + inv_rms * scaled
        - values * cube * jnp.mean(scaled * values, axis=1, keepdims=True)
    ).astype(bf16)
    return (
        grad_hidden,
        grad_router,
        grad_gain,
        grad_gate_mat[None],
        grad_up_mat[None],
        grad_down_mat[None],
    )


def solution(mesh):
    in_specs = (
        P(("dp", "expert"), None),
        P(),
        P(),
        P(("dp", "expert"), None),
        P(("dp", "expert"), None),
        P(("dp", "expert"), None, None),
        P(("dp", "expert"), None, None),
        P(("dp", "expert"), None, None),
    )
    out_specs = (
        P(("dp", "expert"), None),
        P(),
        P(),
        P(("dp", "expert"), None, None),
        P(("dp", "expert"), None, None),
        P(("dp", "expert"), None, None),
    )
    return jax.shard_map(local, mesh=mesh, in_specs=in_specs, out_specs=out_specs, check_vma=False)
```

```python
import jax
import jax.numpy as jnp
from jax import lax
from jax.sharding import PartitionSpec as P


def silu_parts(value):
    sigmoid_v = jax.nn.sigmoid(value)
    return (value * sigmoid_v, sigmoid_v * (1.0 + value * (1.0 - sigmoid_v)))


def dims(left, right, left_dims, right_dims):
    return lax.dot_general(
        left, right, ((left_dims, right_dims), ((), ())), preferred_element_type=jnp.float32
    )


def expert_backward(rows_x, rows_y, prob_rows, gate_mat, up_mat, down_mat):
    slots, chunks, lanes = rows_x.shape
    ff = gate_mat.shape[1]
    gate3 = gate_mat.reshape(chunks, lanes, ff)
    up3 = up_mat.reshape(chunks, lanes, ff)
    down3 = down_mat.reshape(ff, chunks, lanes)
    pre_gate = dims(rows_x, gate3, (1, 2), (0, 1))
    pre_up = dims(rows_x, up3, (1, 2), (0, 1))
    activated, derivative = silu_parts(pre_gate)
    hidden_act = activated * pre_up
    grad_mid = dims(rows_y, down3, (1, 2), (1, 2))
    route_grad = jnp.sum(grad_mid * hidden_act, axis=1).astype(jnp.bfloat16)
    prob_col = prob_rows.astype(jnp.float32)[:, None]
    scaled = prob_col * grad_mid
    grad_pre_gate = (scaled * pre_up * derivative).astype(jnp.bfloat16)
    grad_pre_up = (scaled * activated).astype(jnp.bfloat16)
    scaled_up = (prob_col[:, :, None] * rows_y.astype(jnp.float32)).astype(jnp.bfloat16)
    grad_gate_mat = dims(rows_x, grad_pre_gate, (0,), (0,)).astype(jnp.bfloat16)
    grad_up_mat = dims(rows_x, grad_pre_up, (0,), (0,)).astype(jnp.bfloat16)
    grad_down_mat = dims(hidden_act.astype(jnp.bfloat16), scaled_up, (0,), (0,)).astype(jnp.bfloat16)
    grad_inputs = (
        dims(grad_pre_gate, gate3, (1,), (2,)) + dims(grad_pre_up, up3, (1,), (2,))
    ).astype(jnp.bfloat16)
    return (
        grad_gate_mat.reshape(chunks * lanes, ff),
        grad_up_mat.reshape(chunks * lanes, ff),
        grad_down_mat.reshape(ff, chunks * lanes),
        grad_inputs,
        route_grad,
    )


def local(
    hidden_in, norm_gain, router_weight, grad_out, expert_ids, gate_weight, up_weight, down_weight
):
    f32, bf16 = jnp.float32, jnp.bfloat16
    tok_rows, model_width = hidden_in.shape
    top_count = expert_ids.shape[1]
    experts = router_weight.shape[1]
    capacity = max(2, (tok_rows * top_count * 9 + 8 * experts - 1) // (8 * experts))
    slots = experts * capacity
    routes = tok_rows * top_count
    lanes = 128
    chunks = model_width // lanes
    axes = ("dp", "expert")

    values = hidden_in.astype(f32)
    inv_rms = lax.rsqrt(jnp.mean(values * values, axis=1, keepdims=True) + 1e-06)
    normed = (values * inv_rms * norm_gain).astype(bf16)
    logits = jnp.dot(normed, router_weight, preferred_element_type=f32)
    chosen = expert_ids[:, :, None] == jnp.arange(experts, dtype=jnp.int32)[None, None, :]
    picked = jnp.sum(jnp.where(chosen, logits[:, None, :], 0.0), axis=2)
    route_prob = jax.nn.softmax(picked, axis=1)
    prob_bf = route_prob.astype(bf16)

    flat_ids = expert_ids.reshape(-1)
    onehot = (flat_ids[:, None] == jnp.arange(experts, dtype=jnp.int32)[None, :]).astype(jnp.int32)
    counts = jnp.cumsum(onehot, axis=0)
    slot_idx = jnp.sum(counts * onehot, axis=1) - 1
    target = (flat_ids * capacity + slot_idx).reshape(tok_rows, top_count)
    owner = (
        jnp.full((slots,), routes, jnp.int32)
        .at[target.reshape(-1)]
        .set(jnp.arange(routes, dtype=jnp.int32))
    )
    token_of = jnp.minimum(owner // top_count, tok_rows)
    pad_probs = jnp.concatenate([prob_bf.reshape(-1), jnp.zeros((1,), bf16)], axis=0)
    send_p = pad_probs[owner]

    pad_tile = jnp.zeros((1, chunks, lanes), bf16)
    normed_rows = jnp.concatenate([normed.reshape(tok_rows, chunks, lanes), pad_tile], axis=0)
    grad_rows = jnp.concatenate([grad_out.reshape(tok_rows, chunks, lanes), pad_tile], axis=0)
    send_x = normed_rows[token_of].reshape(experts, capacity, chunks, lanes)
    send_y = grad_rows[token_of].reshape(experts, capacity, chunks, lanes)
    recv_x = lax.all_to_all(send_x, axes, 0, 0, tiled=True).reshape(slots, chunks, lanes)
    recv_y = lax.all_to_all(send_y, axes, 0, 0, tiled=True).reshape(slots, chunks, lanes)
    recv_p = lax.all_to_all(send_p.reshape(experts, capacity), axes, 0, 0, tiled=True)

    grad_gate_mat, grad_up_mat, grad_down_mat, grad_inputs, route_grad = expert_backward(
        recv_x,
        recv_y,
        recv_p.reshape(slots),
        gate_weight[0],
        up_weight[0],
        down_weight[0],
    )
    back_inputs = lax.all_to_all(
        grad_inputs.reshape(experts, capacity, chunks, lanes), axes, 0, 0, tiled=True
    )
    back_grads = lax.all_to_all(route_grad.reshape(experts, capacity), axes, 0, 0, tiled=True)

    back3 = back_inputs.reshape(slots, chunks, lanes)
    route_sum = jnp.sum(back3[target].astype(f32), axis=1).reshape(tok_rows, model_width)
    grad_prob = back_grads.reshape(slots)[target].astype(f32)
    grad_picked = route_prob * (grad_prob - jnp.sum(route_prob * grad_prob, axis=1, keepdims=True))
    grad_logit = jnp.sum(jnp.where(chosen, grad_picked[:, :, None], 0.0), axis=1).astype(bf16)
    router_part = dims(normed, grad_logit, (0,), (0,))
    grad_normed = route_sum + dims(grad_logit, router_weight, (1,), (1,))
    gain_part = jnp.sum(grad_normed * values * inv_rms, axis=0)
    n_dev = experts
    rows_per = model_width // n_dev
    gain_per = model_width // n_dev
    gain_rows = jnp.pad(gain_part.reshape(n_dev, 1, gain_per), ((0, 0), (0, 0), (0, experts - gain_per)))
    send_sum = jnp.concatenate([router_part.reshape(n_dev, rows_per, experts), gain_rows], axis=1)
    part_sum = jnp.sum(lax.all_to_all(send_sum, axes, 0, 0, tiled=True), axis=0)
    whole = lax.all_to_all(
        jnp.broadcast_to(part_sum[None], (n_dev,) + part_sum.shape), axes, 0, 0, tiled=True
    )
    grad_router = whole[:, :rows_per, :].reshape(model_width, experts)
    grad_gain = whole[:, rows_per, :gain_per].reshape(model_width)
    scaled = norm_gain * grad_normed
    cube = inv_rms * inv_rms * inv_rms
    grad_hidden = (
        grad_out.astype(f32)
        + inv_rms * scaled
        - values * cube * jnp.mean(scaled * values, axis=1, keepdims=True)
    ).astype(bf16)
    return (
        grad_hidden,
        grad_router,
        grad_gain,
        grad_gate_mat[None],
        grad_up_mat[None],
        grad_down_mat[None],
    )


def solution(mesh):
    in_specs = (
        P(("dp", "expert"), None),
        P(),
        P(),
        P(("dp", "expert"), None),
        P(("dp", "expert"), None),
        P(("dp", "expert"), None, None),
        P(("dp", "expert"), None, None),
        P(("dp", "expert"), None, None),
    )
    out_specs = (
        P(("dp", "expert"), None),
        P(),
        P(),
        P(("dp", "expert"), None, None),
        P(("dp", "expert"), None, None),
        P(("dp", "expert"), None, None),
    )
    return jax.shard_map(local, mesh=mesh, in_specs=in_specs, out_specs=out_specs, check_vma=False)
```

```python
import jax
import jax.numpy as jnp
from jax import lax
from jax.sharding import PartitionSpec as P


def silu_parts(value):
    sigmoid_v = jax.nn.sigmoid(value)
    return (value * sigmoid_v, sigmoid_v * (1.0 + value * (1.0 - sigmoid_v)))


def dims(left, right, left_dims, right_dims):
    return lax.dot_general(
        left, right, ((left_dims, right_dims), ((), ())), preferred_element_type=jnp.float32
    )


def expert_backward(rows_x, rows_y, prob_rows, gate_mat, up_mat, down_mat):
    slots, chunks, lanes = rows_x.shape
    ff = gate_mat.shape[1]
    gate3 = gate_mat.reshape(chunks, lanes, ff)
    up3 = up_mat.reshape(chunks, lanes, ff)
    down3 = down_mat.reshape(ff, chunks, lanes)
    pre_gate = dims(rows_x, gate3, (1, 2), (0, 1))
    pre_up = dims(rows_x, up3, (1, 2), (0, 1))
    activated, derivative = silu_parts(pre_gate)
    hidden_act = activated * pre_up
    grad_mid = dims(rows_y, down3, (1, 2), (1, 2))
    route_grad = jnp.sum(grad_mid * hidden_act, axis=1).astype(jnp.bfloat16)
    prob_col = prob_rows.astype(jnp.float32)[:, None]
    scaled = prob_col * grad_mid
    grad_pre_gate = (scaled * pre_up * derivative).astype(jnp.bfloat16)
    grad_pre_up = (scaled * activated).astype(jnp.bfloat16)
    scaled_up = (prob_col[:, :, None] * rows_y.astype(jnp.float32)).astype(jnp.bfloat16)
    grad_gate_mat = dims(rows_x, grad_pre_gate, (0,), (0,))
    grad_up_mat = dims(rows_x, grad_pre_up, (0,), (0,))
    grad_down_mat = dims(hidden_act.astype(jnp.bfloat16), scaled_up, (0,), (0,))
    grad_inputs = (
        dims(grad_pre_gate, gate3, (1,), (2,)) + dims(grad_pre_up, up3, (1,), (2,))
    ).astype(jnp.bfloat16)
    return (
        grad_gate_mat.reshape(chunks * lanes, ff),
        grad_up_mat.reshape(chunks * lanes, ff),
        grad_down_mat.reshape(ff, chunks * lanes),
        grad_inputs,
        route_grad,
    )


def local(
    hidden_in, norm_gain, router_weight, grad_out, expert_ids, gate_weight, up_weight, down_weight
):
    f32, bf16 = jnp.float32, jnp.bfloat16
    tok_rows, model_width = hidden_in.shape
    top_count = expert_ids.shape[1]
    experts = router_weight.shape[1]
    capacity = max(2, (tok_rows * top_count * 9 + 8 * experts - 1) // (8 * experts))
    slots = experts * capacity
    routes = tok_rows * top_count
    lanes = 128
    chunks = model_width // lanes
    axes = ("dp", "expert")

    values = hidden_in.astype(f32)
    inv_rms = lax.rsqrt(jnp.mean(values * values, axis=1, keepdims=True) + 1e-06)
    normed = (values * inv_rms * norm_gain).astype(bf16)
    logits = jnp.dot(normed, router_weight, preferred_element_type=f32)
    chosen = expert_ids[:, :, None] == jnp.arange(experts, dtype=jnp.int32)[None, None, :]
    picked = jnp.sum(jnp.where(chosen, logits[:, None, :], 0.0), axis=2)
    route_prob = jax.nn.softmax(picked, axis=1)
    prob_bf = route_prob.astype(bf16)

    flat_ids = expert_ids.reshape(-1)
    onehot = (flat_ids[:, None] == jnp.arange(experts, dtype=jnp.int32)[None, :]).astype(jnp.int32)
    counts = jnp.cumsum(onehot, axis=0)
    slot_idx = jnp.sum(counts * onehot, axis=1) - 1
    target = (flat_ids * capacity + slot_idx).reshape(tok_rows, top_count)
    owner = (
        jnp.full((slots,), routes, jnp.int32)
        .at[target.reshape(-1)]
        .set(jnp.arange(routes, dtype=jnp.int32))
    )
    token_of = jnp.minimum(owner // top_count, tok_rows)
    pad_probs = jnp.concatenate([prob_bf.reshape(-1), jnp.zeros((1,), bf16)], axis=0)
    send_p = pad_probs[owner]

    pad_tile = jnp.zeros((1, chunks, lanes), bf16)
    normed_rows = jnp.concatenate([normed.reshape(tok_rows, chunks, lanes), pad_tile], axis=0)
    grad_rows = jnp.concatenate([grad_out.reshape(tok_rows, chunks, lanes), pad_tile], axis=0)
    send_x = normed_rows[token_of].reshape(experts, capacity, chunks, lanes)
    send_y = grad_rows[token_of].reshape(experts, capacity, chunks, lanes)
    recv_x = lax.all_to_all(send_x, axes, 0, 0, tiled=True)
    recv_y = lax.all_to_all(send_y, axes, 0, 0, tiled=True)
    recv_p = lax.all_to_all(send_p.reshape(experts, capacity), axes, 0, 0, tiled=True)

    half = (capacity + 1) // 2
    sums, back_parts, grad_parts = None, [], []
    for low, high in ((0, half), (half, capacity)):
        width = high - low
        part = expert_backward(
            recv_x[:, low:high].reshape(experts * width, chunks, lanes),
            recv_y[:, low:high].reshape(experts * width, chunks, lanes),
            recv_p[:, low:high].reshape(-1),
            gate_weight[0],
            up_weight[0],
            down_weight[0],
        )
        sums = part[:3] if sums is None else tuple(a + b for a, b in zip(sums, part[:3]))
        back_parts.append(
            lax.all_to_all(
                part[3].reshape(experts, width, chunks, lanes), axes, 0, 0, tiled=True
            )
        )
        grad_parts.append(part[4].reshape(experts, width))
    grad_gate_mat, grad_up_mat, grad_down_mat = (a.astype(bf16) for a in sums)
    back_inputs, slot_grads = lax.optimization_barrier(
        (jnp.concatenate(back_parts, axis=1), jnp.concatenate(grad_parts, axis=1))
    )
    back_grads = lax.all_to_all(slot_grads, axes, 0, 0, tiled=True)

    back3 = back_inputs.reshape(slots, chunks, lanes)
    route_sum = jnp.sum(back3[target].astype(f32), axis=1).reshape(tok_rows, model_width)
    grad_prob = back_grads.reshape(slots)[target].astype(f32)
    grad_picked = route_prob * (grad_prob - jnp.sum(route_prob * grad_prob, axis=1, keepdims=True))
    grad_logit = jnp.sum(jnp.where(chosen, grad_picked[:, :, None], 0.0), axis=1).astype(bf16)
    router_part = dims(normed, grad_logit, (0,), (0,))
    grad_normed = route_sum + dims(grad_logit, router_weight, (1,), (1,))
    gain_part = jnp.sum(grad_normed * values * inv_rms, axis=0)
    n_dev = experts
    rows_per = model_width // n_dev
    gain_per = model_width // n_dev
    gain_rows = jnp.pad(gain_part.reshape(n_dev, 1, gain_per), ((0, 0), (0, 0), (0, experts - gain_per)))
    send_sum = jnp.concatenate([router_part.reshape(n_dev, rows_per, experts), gain_rows], axis=1)
    part_sum = jnp.sum(lax.all_to_all(send_sum, axes, 0, 0, tiled=True), axis=0)
    whole = lax.all_to_all(
        jnp.broadcast_to(part_sum[None], (n_dev,) + part_sum.shape), axes, 0, 0, tiled=True
    )
    grad_router = whole[:, :rows_per, :].reshape(model_width, experts)
    grad_gain = whole[:, rows_per, :gain_per].reshape(model_width)
    scaled = norm_gain * grad_normed
    cube = inv_rms * inv_rms * inv_rms
    grad_hidden = (
        grad_out.astype(f32)
        + inv_rms * scaled
        - values * cube * jnp.mean(scaled * values, axis=1, keepdims=True)
    ).astype(bf16)
    return (
        grad_hidden,
        grad_router,
        grad_gain,
        grad_gate_mat[None],
        grad_up_mat[None],
        grad_down_mat[None],
    )


def solution(mesh):
    in_specs = (
        P(("dp", "expert"), None),
        P(),
        P(),
        P(("dp", "expert"), None),
        P(("dp", "expert"), None),
        P(("dp", "expert"), None, None),
        P(("dp", "expert"), None, None),
        P(("dp", "expert"), None, None),
    )
    out_specs = (
        P(("dp", "expert"), None),
        P(),
        P(),
        P(("dp", "expert"), None, None),
        P(("dp", "expert"), None, None),
        P(("dp", "expert"), None, None),
    )
    return jax.shard_map(local, mesh=mesh, in_specs=in_specs, out_specs=out_specs, check_vma=False)
```

```python
import jax
import jax.numpy as jnp
from jax import lax
from jax.sharding import PartitionSpec as P


def silu_parts(value):
    sigmoid_v = jax.nn.sigmoid(value)
    return (value * sigmoid_v, sigmoid_v * (1.0 + value * (1.0 - sigmoid_v)))


def dims(left, right, left_dims, right_dims):
    return lax.dot_general(
        left, right, ((left_dims, right_dims), ((), ())), preferred_element_type=jnp.float32
    )


def expert_backward(rows_x, rows_y, prob_rows, gate_mat, up_mat, down_mat):
    slots, chunks, lanes = rows_x.shape
    ff = gate_mat.shape[1]
    gate3 = gate_mat.reshape(chunks, lanes, ff)
    up3 = up_mat.reshape(chunks, lanes, ff)
    down3 = down_mat.reshape(ff, chunks, lanes)
    pre_gate = dims(rows_x, gate3, (1, 2), (0, 1))
    pre_up = dims(rows_x, up3, (1, 2), (0, 1))
    activated, derivative = silu_parts(pre_gate)
    hidden_act = activated * pre_up
    grad_mid = dims(rows_y, down3, (1, 2), (1, 2))
    route_grad = jnp.sum(grad_mid * hidden_act, axis=1).astype(jnp.bfloat16)
    prob_col = prob_rows.astype(jnp.float32)[:, None]
    scaled = prob_col * grad_mid
    grad_pre_gate = (scaled * pre_up * derivative).astype(jnp.bfloat16)
    grad_pre_up = (scaled * activated).astype(jnp.bfloat16)
    scaled_up = (prob_col[:, :, None] * rows_y.astype(jnp.float32)).astype(jnp.bfloat16)
    grad_gate_mat = dims(rows_x, grad_pre_gate, (0,), (0,)).astype(jnp.bfloat16)
    grad_up_mat = dims(rows_x, grad_pre_up, (0,), (0,)).astype(jnp.bfloat16)
    grad_down_mat = dims(hidden_act.astype(jnp.bfloat16), scaled_up, (0,), (0,)).astype(jnp.bfloat16)
    grad_inputs = (
        dims(grad_pre_gate, gate3, (1,), (2,)) + dims(grad_pre_up, up3, (1,), (2,))
    ).astype(jnp.bfloat16)
    return (
        grad_gate_mat.reshape(chunks * lanes, ff),
        grad_up_mat.reshape(chunks * lanes, ff),
        grad_down_mat.reshape(ff, chunks * lanes),
        grad_inputs,
        route_grad,
    )


def local(
    hidden_in, norm_gain, router_weight, grad_out, expert_ids, gate_weight, up_weight, down_weight
):
    f32, bf16 = jnp.float32, jnp.bfloat16
    tok_rows, model_width = hidden_in.shape
    top_count = expert_ids.shape[1]
    experts = router_weight.shape[1]
    capacity = max(2, (tok_rows * top_count * 9 + 8 * experts - 1) // (8 * experts))
    slots = experts * capacity
    lanes = 128
    chunks = model_width // lanes
    axes = ("dp", "expert")

    values = hidden_in.astype(f32)
    inv_rms = lax.rsqrt(jnp.mean(values * values, axis=1, keepdims=True) + 1e-06)
    normed = (values * inv_rms * norm_gain).astype(bf16)
    logits = jnp.dot(normed, router_weight, preferred_element_type=f32)
    chosen = expert_ids[:, :, None] == jnp.arange(experts, dtype=jnp.int32)[None, None, :]
    picked = jnp.sum(jnp.where(chosen, logits[:, None, :], 0.0), axis=2)
    route_prob = jax.nn.softmax(picked, axis=1)
    prob_bf = route_prob.astype(bf16)

    flat_ids = expert_ids.reshape(-1)
    onehot = (flat_ids[:, None] == jnp.arange(experts, dtype=jnp.int32)[None, :]).astype(jnp.int32)
    counts = jnp.cumsum(onehot, axis=0)
    slot_idx = jnp.sum(counts * onehot, axis=1) - 1
    target = (flat_ids * capacity + slot_idx).reshape(tok_rows, top_count)
    hit = target[None, :, :] == jnp.arange(slots, dtype=jnp.int32)[:, None, None]
    sel_tok = jnp.any(hit, axis=2).astype(bf16)
    send_p = jnp.sum(jnp.where(hit, prob_bf.astype(f32)[None], 0.0), axis=(1, 2)).astype(bf16)

    normed3 = normed.reshape(tok_rows, chunks, lanes)
    grads3 = grad_out.reshape(tok_rows, chunks, lanes)
    send_x = dims(sel_tok, normed3, (1,), (0,)).astype(bf16).reshape(experts, capacity, chunks, lanes)
    send_y = dims(sel_tok, grads3, (1,), (0,)).astype(bf16).reshape(experts, capacity, chunks, lanes)
    recv_x = lax.all_to_all(send_x, axes, 0, 0, tiled=True)
    recv_y = lax.all_to_all(send_y, axes, 0, 0, tiled=True)
    recv_p = lax.all_to_all(send_p.reshape(experts, capacity), axes, 0, 0, tiled=True)

    grad_gate_mat, grad_up_mat, grad_down_mat, grad_inputs, route_grad = expert_backward(
        recv_x.reshape(slots, chunks, lanes),
        recv_y.reshape(slots, chunks, lanes),
        recv_p.reshape(slots),
        gate_weight[0],
        up_weight[0],
        down_weight[0],
    )
    back_inputs = lax.all_to_all(
        grad_inputs.reshape(experts, capacity, chunks, lanes), axes, 0, 0, tiled=True
    )
    back_grads = lax.all_to_all(route_grad.reshape(experts, capacity), axes, 0, 0, tiled=True)

    route_sum = dims(sel_tok, back_inputs.reshape(slots, chunks, lanes), (0,), (0,)).reshape(
        tok_rows, model_width
    )
    grad_prob = back_grads.reshape(slots)[target].astype(f32)
    grad_picked = route_prob * (grad_prob - jnp.sum(route_prob * grad_prob, axis=1, keepdims=True))
    grad_logit = jnp.sum(jnp.where(chosen, grad_picked[:, :, None], 0.0), axis=1).astype(bf16)
    router_part = dims(normed, grad_logit, (0,), (0,))
    grad_normed = route_sum + dims(grad_logit, router_weight, (1,), (1,))
    gain_part = jnp.sum(grad_normed * values * inv_rms, axis=0)
    n_dev = experts
    rows_per = model_width // n_dev
    gain_per = model_width // n_dev
    gain_rows = jnp.pad(gain_part.reshape(n_dev, 1, gain_per), ((0, 0), (0, 0), (0, experts - gain_per)))
    send_sum = jnp.concatenate([router_part.reshape(n_dev, rows_per, experts), gain_rows], axis=1)
    part_sum = jnp.sum(
        lax.all_to_all(send_sum.astype(bf16), axes, 0, 0, tiled=True).astype(f32), axis=0
    )
    whole = lax.all_to_all(
        jnp.broadcast_to(part_sum[None], (n_dev,) + part_sum.shape), axes, 0, 0, tiled=True
    )
    grad_router = whole[:, :rows_per, :].reshape(model_width, experts)
    grad_gain = whole[:, rows_per, :gain_per].reshape(model_width)
    scaled = norm_gain * grad_normed
    cube = inv_rms * inv_rms * inv_rms
    grad_hidden = (
        grad_out.astype(f32)
        + inv_rms * scaled
        - values * cube * jnp.mean(scaled * values, axis=1, keepdims=True)
    ).astype(bf16)
    return (
        grad_hidden,
        grad_router,
        grad_gain,
        grad_gate_mat[None],
        grad_up_mat[None],
        grad_down_mat[None],
    )


def solution(mesh):
    in_specs = (
        P(("dp", "expert"), None),
        P(),
        P(),
        P(("dp", "expert"), None),
        P(("dp", "expert"), None),
        P(("dp", "expert"), None, None),
        P(("dp", "expert"), None, None),
        P(("dp", "expert"), None, None),
    )
    out_specs = (
        P(("dp", "expert"), None),
        P(),
        P(),
        P(("dp", "expert"), None, None),
        P(("dp", "expert"), None, None),
        P(("dp", "expert"), None, None),
    )
    return jax.shard_map(local, mesh=mesh, in_specs=in_specs, out_specs=out_specs, check_vma=False)
```

```python
import jax
import jax.numpy as jnp
from jax import lax
from jax.sharding import PartitionSpec as P


def silu_parts(value):
    sigmoid_v = jax.nn.sigmoid(value)
    return (value * sigmoid_v, sigmoid_v * (1.0 + value * (1.0 - sigmoid_v)))


def dims(left, right, left_dims, right_dims):
    return lax.dot_general(
        left, right, ((left_dims, right_dims), ((), ())), preferred_element_type=jnp.float32
    )


def expert_backward(rows_x, rows_y, prob_rows, gate_mat, up_mat, down_mat):
    slots, chunks, lanes = rows_x.shape
    ff = gate_mat.shape[1]
    gate3 = gate_mat.reshape(chunks, lanes, ff)
    up3 = up_mat.reshape(chunks, lanes, ff)
    down3 = down_mat.reshape(ff, chunks, lanes)
    pre_gate = dims(rows_x, gate3, (1, 2), (0, 1))
    pre_up = dims(rows_x, up3, (1, 2), (0, 1))
    activated, derivative = silu_parts(pre_gate)
    hidden_act = activated * pre_up
    grad_mid = dims(rows_y, down3, (1, 2), (1, 2))
    route_grad = jnp.sum(grad_mid * hidden_act, axis=1).astype(jnp.bfloat16)
    prob_col = prob_rows.astype(jnp.float32)[:, None]
    scaled = prob_col * grad_mid
    grad_pre_gate = (scaled * pre_up * derivative).astype(jnp.bfloat16)
    grad_pre_up = (scaled * activated).astype(jnp.bfloat16)
    scaled_up = (prob_col[:, :, None] * rows_y.astype(jnp.float32)).astype(jnp.bfloat16)
    grad_gate_mat = dims(rows_x, grad_pre_gate, (0,), (0,)).astype(jnp.bfloat16)
    grad_up_mat = dims(rows_x, grad_pre_up, (0,), (0,)).astype(jnp.bfloat16)
    grad_down_mat = dims(hidden_act.astype(jnp.bfloat16), scaled_up, (0,), (0,)).astype(jnp.bfloat16)
    grad_inputs = (
        dims(grad_pre_gate, gate3, (1,), (2,)) + dims(grad_pre_up, up3, (1,), (2,))
    ).astype(jnp.bfloat16)
    return (
        grad_gate_mat.reshape(chunks * lanes, ff),
        grad_up_mat.reshape(chunks * lanes, ff),
        grad_down_mat.reshape(ff, chunks * lanes),
        grad_inputs,
        route_grad,
    )


def local(
    hidden_in, norm_gain, router_weight, grad_out, expert_ids, gate_weight, up_weight, down_weight
):
    f32, bf16 = jnp.float32, jnp.bfloat16
    tok_rows, model_width = hidden_in.shape
    top_count = expert_ids.shape[1]
    experts = router_weight.shape[1]
    capacity = max(2, (tok_rows * top_count * 9 + 8 * experts - 1) // (8 * experts))
    slots = experts * capacity
    lanes = 128
    chunks = model_width // lanes
    axes = ("dp", "expert")

    values = hidden_in.astype(f32)
    inv_rms = lax.rsqrt(jnp.mean(values * values, axis=1, keepdims=True) + 1e-06)
    normed = (values * inv_rms * norm_gain).astype(bf16)
    logits = jnp.dot(normed, router_weight, preferred_element_type=f32)
    chosen = expert_ids[:, :, None] == jnp.arange(experts, dtype=jnp.int32)[None, None, :]
    picked = jnp.sum(jnp.where(chosen, logits[:, None, :], 0.0), axis=2)
    route_prob = jax.nn.softmax(picked, axis=1)
    prob_bf = route_prob.astype(bf16)

    flat_ids = expert_ids.reshape(-1)
    onehot = (flat_ids[:, None] == jnp.arange(experts, dtype=jnp.int32)[None, :]).astype(jnp.int32)
    counts = jnp.cumsum(onehot, axis=0)
    slot_idx = jnp.sum(counts * onehot, axis=1) - 1
    target = (flat_ids * capacity + slot_idx).reshape(tok_rows, top_count)
    hit = target[None, :, :] == jnp.arange(slots, dtype=jnp.int32)[:, None, None]
    sel_tok = jnp.any(hit, axis=2).astype(bf16)
    send_p = jnp.sum(jnp.where(hit, prob_bf.astype(f32)[None], 0.0), axis=(1, 2)).astype(bf16)

    normed3 = normed.reshape(tok_rows, chunks, lanes)
    grads3 = grad_out.reshape(tok_rows, chunks, lanes)
    send_x = dims(sel_tok, normed3, (1,), (0,)).astype(bf16).reshape(experts, capacity, chunks, lanes)
    send_y = dims(sel_tok, grads3, (1,), (0,)).astype(bf16).reshape(experts, capacity, chunks, lanes)
    recv_x = lax.all_to_all(send_x, axes, 0, 0, tiled=True)
    recv_y = lax.all_to_all(send_y, axes, 0, 0, tiled=True)
    recv_p = lax.all_to_all(send_p.reshape(experts, capacity), axes, 0, 0, tiled=True)

    grad_gate_mat, grad_up_mat, grad_down_mat, grad_inputs, route_grad = expert_backward(
        recv_x.reshape(slots, chunks, lanes),
        recv_y.reshape(slots, chunks, lanes),
        recv_p.reshape(slots),
        gate_weight[0],
        up_weight[0],
        down_weight[0],
    )
    back_inputs = lax.all_to_all(
        grad_inputs.reshape(experts, capacity, chunks, lanes), axes, 0, 0, tiled=True
    )
    back_grads = lax.all_to_all(route_grad.reshape(experts, capacity), axes, 0, 0, tiled=True)

    route_sum = dims(sel_tok, back_inputs.reshape(slots, chunks, lanes), (0,), (0,)).reshape(
        tok_rows, model_width
    )
    grad_prob = back_grads.reshape(slots)[target].astype(f32)
    grad_picked = route_prob * (grad_prob - jnp.sum(route_prob * grad_prob, axis=1, keepdims=True))
    grad_logit = jnp.sum(jnp.where(chosen, grad_picked[:, :, None], 0.0), axis=1).astype(bf16)
    router_part = dims(normed, grad_logit, (0,), (0,))
    grad_normed = route_sum + dims(grad_logit, router_weight, (1,), (1,))
    gain_part = jnp.sum(grad_normed * values * inv_rms, axis=0)
    n_dev = experts
    rows_per = model_width // n_dev
    gain_per = model_width // n_dev
    gain_rows = jnp.pad(gain_part.reshape(n_dev, 1, gain_per), ((0, 0), (0, 0), (0, experts - gain_per)))
    send_sum = jnp.concatenate([router_part.reshape(n_dev, rows_per, experts), gain_rows], axis=1)
    part_sum = jnp.sum(
        lax.all_to_all(send_sum.astype(bf16), axes, 0, 0, tiled=True).astype(f32), axis=0
    )
    whole = lax.all_to_all(
        jnp.broadcast_to(part_sum.astype(bf16)[None], (n_dev,) + part_sum.shape),
        axes,
        0,
        0,
        tiled=True,
    ).astype(f32)
    grad_router = whole[:, :rows_per, :].reshape(model_width, experts)
    grad_gain = whole[:, rows_per, :gain_per].reshape(model_width)
    scaled = norm_gain * grad_normed
    cube = inv_rms * inv_rms * inv_rms
    grad_hidden = (
        grad_out.astype(f32)
        + inv_rms * scaled
        - values * cube * jnp.mean(scaled * values, axis=1, keepdims=True)
    ).astype(bf16)
    return (
        grad_hidden,
        grad_router,
        grad_gain,
        grad_gate_mat[None],
        grad_up_mat[None],
        grad_down_mat[None],
    )


def solution(mesh):
    in_specs = (
        P(("dp", "expert"), None),
        P(),
        P(),
        P(("dp", "expert"), None),
        P(("dp", "expert"), None),
        P(("dp", "expert"), None, None),
        P(("dp", "expert"), None, None),
        P(("dp", "expert"), None, None),
    )
    out_specs = (
        P(("dp", "expert"), None),
        P(),
        P(),
        P(("dp", "expert"), None, None),
        P(("dp", "expert"), None, None),
        P(("dp", "expert"), None, None),
    )
    return jax.shard_map(local, mesh=mesh, in_specs=in_specs, out_specs=out_specs, check_vma=False)
```

```python
import jax
import jax.numpy as jnp
from jax import lax
from jax.sharding import PartitionSpec as P


def silu_parts(value):
    sigmoid_v = jax.nn.sigmoid(value)
    return (value * sigmoid_v, sigmoid_v * (1.0 + value * (1.0 - sigmoid_v)))


def dims(left, right, left_dims, right_dims):
    return lax.dot_general(
        left, right, ((left_dims, right_dims), ((), ())), preferred_element_type=jnp.float32
    )


def expert_backward(rows_x, rows_y, prob_rows, gate_mat, up_mat, down_mat):
    slots, chunks, lanes = rows_x.shape
    ff = gate_mat.shape[1]
    gate3 = gate_mat.reshape(chunks, lanes, ff)
    up3 = up_mat.reshape(chunks, lanes, ff)
    down3 = down_mat.reshape(ff, chunks, lanes)
    pre_gate = dims(rows_x, gate3, (1, 2), (0, 1))
    pre_up = dims(rows_x, up3, (1, 2), (0, 1))
    activated, derivative = silu_parts(pre_gate)
    hidden_act = activated * pre_up
    grad_mid = dims(rows_y, down3, (1, 2), (1, 2))
    route_grad = jnp.sum(grad_mid * hidden_act, axis=1).astype(jnp.bfloat16)
    prob_col = prob_rows.astype(jnp.float32)[:, None]
    scaled = prob_col * grad_mid
    grad_pre_gate = (scaled * pre_up * derivative).astype(jnp.bfloat16)
    grad_pre_up = (scaled * activated).astype(jnp.bfloat16)
    scaled_up = (prob_col[:, :, None] * rows_y.astype(jnp.float32)).astype(jnp.bfloat16)
    grad_gate_mat = dims(rows_x, grad_pre_gate, (0,), (0,)).astype(jnp.bfloat16)
    grad_up_mat = dims(rows_x, grad_pre_up, (0,), (0,)).astype(jnp.bfloat16)
    grad_down_mat = dims(hidden_act.astype(jnp.bfloat16), scaled_up, (0,), (0,)).astype(jnp.bfloat16)
    grad_inputs = (
        (dims(grad_pre_gate, gate_mat, (1,), (1,)) + dims(grad_pre_up, up_mat, (1,), (1,)))
        .astype(jnp.bfloat16)
        .reshape(slots, chunks, lanes)
    )
    return (
        grad_gate_mat.reshape(chunks * lanes, ff),
        grad_up_mat.reshape(chunks * lanes, ff),
        grad_down_mat.reshape(ff, chunks * lanes),
        grad_inputs,
        route_grad,
    )


def local(
    hidden_in, norm_gain, router_weight, grad_out, expert_ids, gate_weight, up_weight, down_weight
):
    f32, bf16 = jnp.float32, jnp.bfloat16
    tok_rows, model_width = hidden_in.shape
    top_count = expert_ids.shape[1]
    experts = router_weight.shape[1]
    capacity = max(2, (tok_rows * top_count * 9 + 8 * experts - 1) // (8 * experts))
    slots = experts * capacity
    lanes = 128
    chunks = model_width // lanes
    axes = ("dp", "expert")

    values = hidden_in.astype(f32)
    inv_rms = lax.rsqrt(jnp.mean(values * values, axis=1, keepdims=True) + 1e-06)
    normed = (values * inv_rms * norm_gain).astype(bf16)
    logits = jnp.dot(normed, router_weight, preferred_element_type=f32)
    chosen = expert_ids[:, :, None] == jnp.arange(experts, dtype=jnp.int32)[None, None, :]
    picked = jnp.sum(jnp.where(chosen, logits[:, None, :], 0.0), axis=2)
    route_prob = jax.nn.softmax(picked, axis=1)
    prob_bf = route_prob.astype(bf16)

    flat_ids = expert_ids.reshape(-1)
    onehot = (flat_ids[:, None] == jnp.arange(experts, dtype=jnp.int32)[None, :]).astype(jnp.int32)
    counts = jnp.cumsum(onehot, axis=0)
    slot_idx = jnp.sum(counts * onehot, axis=1) - 1
    target = (flat_ids * capacity + slot_idx).reshape(tok_rows, top_count)
    hit = target[None, :, :] == jnp.arange(slots, dtype=jnp.int32)[:, None, None]
    sel_tok = jnp.any(hit, axis=2).astype(bf16)
    send_p = jnp.sum(jnp.where(hit, prob_bf.astype(f32)[None], 0.0), axis=(1, 2)).astype(bf16)

    normed3 = normed.reshape(tok_rows, chunks, lanes)
    grads3 = grad_out.reshape(tok_rows, chunks, lanes)
    send_x = dims(sel_tok, normed3, (1,), (0,)).astype(bf16).reshape(experts, capacity, chunks, lanes)
    send_y = dims(sel_tok, grads3, (1,), (0,)).astype(bf16).reshape(experts, capacity, chunks, lanes)
    recv_x = lax.all_to_all(send_x, axes, 0, 0, tiled=True)
    recv_y = lax.all_to_all(send_y, axes, 0, 0, tiled=True)
    recv_p = lax.all_to_all(send_p.reshape(experts, capacity), axes, 0, 0, tiled=True)

    grad_gate_mat, grad_up_mat, grad_down_mat, grad_inputs, route_grad = expert_backward(
        recv_x.reshape(slots, chunks, lanes),
        recv_y.reshape(slots, chunks, lanes),
        recv_p.reshape(slots),
        gate_weight[0],
        up_weight[0],
        down_weight[0],
    )
    back_inputs = lax.all_to_all(
        grad_inputs.reshape(experts, capacity, chunks, lanes), axes, 0, 0, tiled=True
    )
    back_grads = lax.all_to_all(route_grad.reshape(experts, capacity), axes, 0, 0, tiled=True)

    route_sum = dims(sel_tok, back_inputs.reshape(slots, chunks, lanes), (0,), (0,)).reshape(
        tok_rows, model_width
    )
    grad_prob = back_grads.reshape(slots)[target].astype(f32)
    grad_picked = route_prob * (grad_prob - jnp.sum(route_prob * grad_prob, axis=1, keepdims=True))
    grad_logit = jnp.sum(jnp.where(chosen, grad_picked[:, :, None], 0.0), axis=1).astype(bf16)
    router_part = dims(normed, grad_logit, (0,), (0,))
    grad_normed = route_sum + dims(grad_logit, router_weight, (1,), (1,))
    gain_part = jnp.sum(grad_normed * values * inv_rms, axis=0)
    n_dev = experts
    rows_per = model_width // n_dev
    gain_per = model_width // n_dev
    gain_rows = jnp.pad(gain_part.reshape(n_dev, 1, gain_per), ((0, 0), (0, 0), (0, experts - gain_per)))
    send_sum = jnp.concatenate([router_part.reshape(n_dev, rows_per, experts), gain_rows], axis=1)
    part_sum = jnp.sum(
        lax.all_to_all(send_sum.astype(bf16), axes, 0, 0, tiled=True).astype(f32), axis=0
    )
    whole = lax.all_to_all(
        jnp.broadcast_to(part_sum.astype(bf16)[None], (n_dev,) + part_sum.shape),
        axes,
        0,
        0,
        tiled=True,
    ).astype(f32)
    grad_router = whole[:, :rows_per, :].reshape(model_width, experts)
    grad_gain = whole[:, rows_per, :gain_per].reshape(model_width)
    scaled = norm_gain * grad_normed
    cube = inv_rms * inv_rms * inv_rms
    grad_hidden = (
        grad_out.astype(f32)
        + inv_rms * scaled
        - values * cube * jnp.mean(scaled * values, axis=1, keepdims=True)
    ).astype(bf16)
    return (
        grad_hidden,
        grad_router,
        grad_gain,
        grad_gate_mat[None],
        grad_up_mat[None],
        grad_down_mat[None],
    )


def solution(mesh):
    in_specs = (
        P(("dp", "expert"), None),
        P(),
        P(),
        P(("dp", "expert"), None),
        P(("dp", "expert"), None),
        P(("dp", "expert"), None, None),
        P(("dp", "expert"), None, None),
        P(("dp", "expert"), None, None),
    )
    out_specs = (
        P(("dp", "expert"), None),
        P(),
        P(),
        P(("dp", "expert"), None, None),
        P(("dp", "expert"), None, None),
        P(("dp", "expert"), None, None),
    )
    return jax.shard_map(local, mesh=mesh, in_specs=in_specs, out_specs=out_specs, check_vma=False)
```

```python
import jax
import jax.numpy as jnp
from jax import lax
from jax.sharding import PartitionSpec as P


def silu_parts(value):
    sigmoid_v = jax.nn.sigmoid(value)
    return (value * sigmoid_v, sigmoid_v * (1.0 + value * (1.0 - sigmoid_v)))


def dims(left, right, left_dims, right_dims):
    return lax.dot_general(
        left, right, ((left_dims, right_dims), ((), ())), preferred_element_type=jnp.float32
    )


def expert_backward(rows_x, rows_y, prob_rows, gate_mat, up_mat, down_mat):
    slots, chunks, lanes = rows_x.shape
    ff = gate_mat.shape[1]
    gate3 = gate_mat.reshape(chunks, lanes, ff)
    up3 = up_mat.reshape(chunks, lanes, ff)
    down3 = down_mat.reshape(ff, chunks, lanes)
    pre_gate = dims(rows_x, gate3, (1, 2), (0, 1))
    pre_up = dims(rows_x, up3, (1, 2), (0, 1))
    activated, derivative = silu_parts(pre_gate)
    hidden_act = activated * pre_up
    grad_mid = dims(rows_y, down3, (1, 2), (1, 2))
    route_grad = jnp.sum(grad_mid * hidden_act, axis=1).astype(jnp.bfloat16)
    prob_col = prob_rows.astype(jnp.float32)[:, None]
    scaled = prob_col * grad_mid
    grad_pre_gate = (scaled * pre_up * derivative).astype(jnp.bfloat16)
    grad_pre_up = (scaled * activated).astype(jnp.bfloat16)
    scaled_up = (prob_col[:, :, None] * rows_y.astype(jnp.float32)).astype(jnp.bfloat16)
    grad_gate_mat = dims(rows_x, grad_pre_gate, (0,), (0,)).astype(jnp.bfloat16)
    grad_up_mat = dims(rows_x, grad_pre_up, (0,), (0,)).astype(jnp.bfloat16)
    grad_down_mat = dims(hidden_act.astype(jnp.bfloat16), scaled_up, (0,), (0,)).astype(jnp.bfloat16)
    grad_inputs = (
        (dims(grad_pre_gate, gate_mat, (1,), (1,)) + dims(grad_pre_up, up_mat, (1,), (1,)))
        .astype(jnp.bfloat16)
        .reshape(slots, chunks, lanes)
    )
    return (
        grad_gate_mat.reshape(chunks * lanes, ff),
        grad_up_mat.reshape(chunks * lanes, ff),
        grad_down_mat.reshape(ff, chunks * lanes),
        grad_inputs,
        route_grad,
    )


def local(
    hidden_in, norm_gain, router_weight, grad_out, expert_ids, gate_weight, up_weight, down_weight
):
    f32, bf16 = jnp.float32, jnp.bfloat16
    tok_rows, model_width = hidden_in.shape
    top_count = expert_ids.shape[1]
    experts = router_weight.shape[1]
    capacity = max(2, (tok_rows * top_count * 9 + 8 * experts - 1) // (8 * experts))
    slots = experts * capacity
    lanes = 128
    chunks = model_width // lanes
    axes = ("dp", "expert")

    values = hidden_in.astype(f32)
    inv_rms = lax.rsqrt(jnp.mean(values * values, axis=1, keepdims=True) + 1e-06)
    normed = (values * inv_rms * norm_gain).astype(bf16)
    logits = jnp.dot(normed, router_weight, preferred_element_type=f32)
    chosen = expert_ids[:, :, None] == jnp.arange(experts, dtype=jnp.int32)[None, None, :]
    picked = jnp.sum(jnp.where(chosen, logits[:, None, :], 0.0), axis=2)
    route_prob = jax.nn.softmax(picked, axis=1)
    prob_bf = route_prob.astype(bf16)

    flat_ids = expert_ids.reshape(-1)
    onehot = (flat_ids[:, None] == jnp.arange(experts, dtype=jnp.int32)[None, :]).astype(jnp.int32)
    counts = jnp.cumsum(onehot, axis=0)
    slot_idx = jnp.sum(counts * onehot, axis=1) - 1
    target = (flat_ids * capacity + slot_idx).reshape(tok_rows, top_count)
    hit = target[None, :, :] == jnp.arange(slots, dtype=jnp.int32)[:, None, None]
    sel_tok = jnp.any(hit, axis=2).astype(bf16)
    send_p = jnp.sum(jnp.where(hit, prob_bf.astype(f32)[None], 0.0), axis=(1, 2)).astype(bf16)

    send_x = dims(sel_tok, normed, (1,), (0,)).astype(bf16).reshape(experts, capacity, chunks, lanes)
    send_y = dims(sel_tok, grad_out, (1,), (0,)).astype(bf16).reshape(experts, capacity, chunks, lanes)
    recv_x = lax.all_to_all(send_x, axes, 0, 0, tiled=True)
    recv_y = lax.all_to_all(send_y, axes, 0, 0, tiled=True)
    recv_p = lax.all_to_all(send_p.reshape(experts, capacity), axes, 0, 0, tiled=True)

    grad_gate_mat, grad_up_mat, grad_down_mat, grad_inputs, route_grad = expert_backward(
        recv_x.reshape(slots, chunks, lanes),
        recv_y.reshape(slots, chunks, lanes),
        recv_p.reshape(slots),
        gate_weight[0],
        up_weight[0],
        down_weight[0],
    )
    back_inputs = lax.all_to_all(
        grad_inputs.reshape(experts, capacity, chunks, lanes), axes, 0, 0, tiled=True
    )
    back_grads = lax.all_to_all(route_grad.reshape(experts, capacity), axes, 0, 0, tiled=True)

    route_sum = dims(sel_tok, back_inputs.reshape(slots, chunks, lanes), (0,), (0,)).reshape(
        tok_rows, model_width
    )
    grad_prob = back_grads.reshape(slots)[target].astype(f32)
    grad_picked = route_prob * (grad_prob - jnp.sum(route_prob * grad_prob, axis=1, keepdims=True))
    grad_logit = jnp.sum(jnp.where(chosen, grad_picked[:, :, None], 0.0), axis=1).astype(bf16)
    router_part = dims(normed, grad_logit, (0,), (0,))
    grad_normed = route_sum + dims(grad_logit, router_weight, (1,), (1,))
    gain_part = jnp.sum(grad_normed * values * inv_rms, axis=0)
    n_dev = experts
    rows_per = model_width // n_dev
    gain_per = model_width // n_dev
    gain_rows = jnp.pad(gain_part.reshape(n_dev, 1, gain_per), ((0, 0), (0, 0), (0, experts - gain_per)))
    send_sum = jnp.concatenate([router_part.reshape(n_dev, rows_per, experts), gain_rows], axis=1)
    part_sum = jnp.sum(
        lax.all_to_all(send_sum.astype(bf16), axes, 0, 0, tiled=True).astype(f32), axis=0
    )
    whole = lax.all_to_all(
        jnp.broadcast_to(part_sum.astype(bf16)[None], (n_dev,) + part_sum.shape),
        axes,
        0,
        0,
        tiled=True,
    ).astype(f32)
    grad_router = whole[:, :rows_per, :].reshape(model_width, experts)
    grad_gain = whole[:, rows_per, :gain_per].reshape(model_width)
    scaled = norm_gain * grad_normed
    cube = inv_rms * inv_rms * inv_rms
    grad_hidden = (
        grad_out.astype(f32)
        + inv_rms * scaled
        - values * cube * jnp.mean(scaled * values, axis=1, keepdims=True)
    ).astype(bf16)
    return (
        grad_hidden,
        grad_router,
        grad_gain,
        grad_gate_mat[None],
        grad_up_mat[None],
        grad_down_mat[None],
    )


def solution(mesh):
    in_specs = (
        P(("dp", "expert"), None),
        P(),
        P(),
        P(("dp", "expert"), None),
        P(("dp", "expert"), None),
        P(("dp", "expert"), None, None),
        P(("dp", "expert"), None, None),
        P(("dp", "expert"), None, None),
    )
    out_specs = (
        P(("dp", "expert"), None),
        P(),
        P(),
        P(("dp", "expert"), None, None),
        P(("dp", "expert"), None, None),
        P(("dp", "expert"), None, None),
    )
    return jax.shard_map(local, mesh=mesh, in_specs=in_specs, out_specs=out_specs, check_vma=False)
```

```python
import jax
import jax.numpy as jnp
from jax import lax
from jax.sharding import PartitionSpec as P


def silu_parts(value):
    sigmoid_v = jax.nn.sigmoid(value)
    return (value * sigmoid_v, sigmoid_v * (1.0 + value * (1.0 - sigmoid_v)))


def dims(left, right, left_dims, right_dims):
    return lax.dot_general(
        left, right, ((left_dims, right_dims), ((), ())), preferred_element_type=jnp.float32
    )


def expert_backward(rows_x, rows_y, prob_rows, gate_mat, up_mat, down_mat):
    slots, chunks, lanes = rows_x.shape
    rows_x = rows_x.reshape(slots, chunks * lanes)
    rows_y = rows_y.reshape(slots, chunks * lanes)
    pre_gate = jnp.dot(rows_x, gate_mat, preferred_element_type=jnp.float32)
    pre_up = jnp.dot(rows_x, up_mat, preferred_element_type=jnp.float32)
    activated, derivative = silu_parts(pre_gate)
    hidden_act = activated * pre_up
    grad_mid = dims(rows_y, down_mat, (1,), (1,))
    route_grad = jnp.sum(grad_mid * hidden_act, axis=1).astype(jnp.bfloat16)
    prob_col = prob_rows.astype(jnp.float32)[:, None]
    scaled = prob_col * grad_mid
    grad_pre_gate = (scaled * pre_up * derivative).astype(jnp.bfloat16)
    grad_pre_up = (scaled * activated).astype(jnp.bfloat16)
    scaled_up = (prob_col * rows_y.astype(jnp.float32)).astype(jnp.bfloat16)
    grad_gate_mat = dims(rows_x, grad_pre_gate, (0,), (0,)).astype(jnp.bfloat16)
    grad_up_mat = dims(rows_x, grad_pre_up, (0,), (0,)).astype(jnp.bfloat16)
    grad_down_mat = dims(hidden_act.astype(jnp.bfloat16), scaled_up, (0,), (0,)).astype(jnp.bfloat16)
    grad_inputs = (
        (dims(grad_pre_gate, gate_mat, (1,), (1,)) + dims(grad_pre_up, up_mat, (1,), (1,)))
        .astype(jnp.bfloat16)
        .reshape(slots, chunks, lanes)
    )
    return (grad_gate_mat, grad_up_mat, grad_down_mat, grad_inputs, route_grad)


def local(
    hidden_in, norm_gain, router_weight, grad_out, expert_ids, gate_weight, up_weight, down_weight
):
    f32, bf16 = jnp.float32, jnp.bfloat16
    tok_rows, model_width = hidden_in.shape
    top_count = expert_ids.shape[1]
    experts = router_weight.shape[1]
    capacity = max(2, (tok_rows * top_count * 9 + 8 * experts - 1) // (8 * experts))
    slots = experts * capacity
    lanes = 128
    chunks = model_width // lanes
    axes = ("dp", "expert")

    values = hidden_in.astype(f32)
    inv_rms = lax.rsqrt(jnp.mean(values * values, axis=1, keepdims=True) + 1e-06)
    normed = (values * inv_rms * norm_gain).astype(bf16)
    logits = jnp.dot(normed, router_weight, preferred_element_type=f32)
    chosen = expert_ids[:, :, None] == jnp.arange(experts, dtype=jnp.int32)[None, None, :]
    picked = jnp.sum(jnp.where(chosen, logits[:, None, :], 0.0), axis=2)
    route_prob = jax.nn.softmax(picked, axis=1)
    prob_bf = route_prob.astype(bf16)

    flat_ids = expert_ids.reshape(-1)
    onehot = (flat_ids[:, None] == jnp.arange(experts, dtype=jnp.int32)[None, :]).astype(jnp.int32)
    counts = jnp.cumsum(onehot, axis=0)
    slot_idx = jnp.sum(counts * onehot, axis=1) - 1
    target = (flat_ids * capacity + slot_idx).reshape(tok_rows, top_count)
    hit = target[None, :, :] == jnp.arange(slots, dtype=jnp.int32)[:, None, None]
    sel_tok = jnp.any(hit, axis=2).astype(bf16)
    send_p = jnp.sum(jnp.where(hit, prob_bf.astype(f32)[None], 0.0), axis=(1, 2)).astype(bf16)

    send_x = dims(sel_tok, normed, (1,), (0,)).astype(bf16).reshape(experts, capacity, chunks, lanes)
    send_y = dims(sel_tok, grad_out, (1,), (0,)).astype(bf16).reshape(experts, capacity, chunks, lanes)
    recv_x = lax.all_to_all(send_x, axes, 0, 0, tiled=True)
    recv_y = lax.all_to_all(send_y, axes, 0, 0, tiled=True)
    recv_p = lax.all_to_all(send_p.reshape(experts, capacity), axes, 0, 0, tiled=True)

    grad_gate_mat, grad_up_mat, grad_down_mat, grad_inputs, route_grad = expert_backward(
        recv_x.reshape(slots, chunks, lanes),
        recv_y.reshape(slots, chunks, lanes),
        recv_p.reshape(slots),
        gate_weight[0],
        up_weight[0],
        down_weight[0],
    )
    back_inputs = lax.all_to_all(
        grad_inputs.reshape(experts, capacity, chunks, lanes), axes, 0, 0, tiled=True
    )
    back_grads = lax.all_to_all(route_grad.reshape(experts, capacity), axes, 0, 0, tiled=True)

    route_sum = dims(sel_tok, back_inputs.reshape(slots, model_width), (0,), (0,))
    grad_prob = back_grads.reshape(slots)[target].astype(f32)
    grad_picked = route_prob * (grad_prob - jnp.sum(route_prob * grad_prob, axis=1, keepdims=True))
    grad_logit = jnp.sum(jnp.where(chosen, grad_picked[:, :, None], 0.0), axis=1).astype(bf16)
    router_part = dims(normed, grad_logit, (0,), (0,))
    grad_normed = route_sum + dims(grad_logit, router_weight, (1,), (1,))
    gain_part = jnp.sum(grad_normed * values * inv_rms, axis=0)
    n_dev = experts
    rows_per = model_width // n_dev
    gain_per = model_width // n_dev
    gain_rows = jnp.pad(gain_part.reshape(n_dev, 1, gain_per), ((0, 0), (0, 0), (0, experts - gain_per)))
    send_sum = jnp.concatenate([router_part.reshape(n_dev, rows_per, experts), gain_rows], axis=1)
    part_sum = jnp.sum(
        lax.all_to_all(send_sum.astype(bf16), axes, 0, 0, tiled=True).astype(f32), axis=0
    )
    whole = lax.all_to_all(
        jnp.broadcast_to(part_sum.astype(bf16)[None], (n_dev,) + part_sum.shape),
        axes,
        0,
        0,
        tiled=True,
    ).astype(f32)
    grad_router = whole[:, :rows_per, :].reshape(model_width, experts)
    grad_gain = whole[:, rows_per, :gain_per].reshape(model_width)
    scaled = norm_gain * grad_normed
    cube = inv_rms * inv_rms * inv_rms
    grad_hidden = (
        grad_out.astype(f32)
        + inv_rms * scaled
        - values * cube * jnp.mean(scaled * values, axis=1, keepdims=True)
    ).astype(bf16)
    return (
        grad_hidden,
        grad_router,
        grad_gain,
        grad_gate_mat[None],
        grad_up_mat[None],
        grad_down_mat[None],
    )


def solution(mesh):
    in_specs = (
        P(("dp", "expert"), None),
        P(),
        P(),
        P(("dp", "expert"), None),
        P(("dp", "expert"), None),
        P(("dp", "expert"), None, None),
        P(("dp", "expert"), None, None),
        P(("dp", "expert"), None, None),
    )
    out_specs = (
        P(("dp", "expert"), None),
        P(),
        P(),
        P(("dp", "expert"), None, None),
        P(("dp", "expert"), None, None),
        P(("dp", "expert"), None, None),
    )
    return jax.shard_map(local, mesh=mesh, in_specs=in_specs, out_specs=out_specs, check_vma=False)
```

```python
import jax
import jax.numpy as jnp
from jax import lax
from jax.sharding import PartitionSpec as P


def silu_parts(value):
    sigmoid_v = jax.nn.sigmoid(value)
    return (value * sigmoid_v, sigmoid_v * (1.0 + value * (1.0 - sigmoid_v)))


def dims(left, right, left_dims, right_dims):
    return lax.dot_general(
        left, right, ((left_dims, right_dims), ((), ())), preferred_element_type=jnp.float32
    )


def expert_backward(rows_x, rows_y, prob_rows, gate_mat, up_mat, down_mat):
    slots, chunks, lanes = rows_x.shape
    rows_x = rows_x.reshape(slots, chunks * lanes)
    rows_y = rows_y.reshape(slots, chunks * lanes)
    pre_gate = jnp.dot(rows_x, gate_mat, preferred_element_type=jnp.float32)
    pre_up = jnp.dot(rows_x, up_mat, preferred_element_type=jnp.float32)
    activated, derivative = silu_parts(pre_gate)
    hidden_act = activated * pre_up
    grad_mid = dims(rows_y, down_mat, (1,), (1,))
    route_grad = jnp.sum(grad_mid * hidden_act, axis=1).astype(jnp.bfloat16)
    prob_col = prob_rows.astype(jnp.float32)[:, None]
    scaled = prob_col * grad_mid
    grad_pre_gate = (scaled * pre_up * derivative).astype(jnp.bfloat16)
    grad_pre_up = (scaled * activated).astype(jnp.bfloat16)
    scaled_up = (prob_col * rows_y.astype(jnp.float32)).astype(jnp.bfloat16)
    grad_gate_mat = dims(rows_x, grad_pre_gate, (0,), (0,)).astype(jnp.bfloat16)
    grad_up_mat = dims(rows_x, grad_pre_up, (0,), (0,)).astype(jnp.bfloat16)
    grad_down_mat = dims(hidden_act.astype(jnp.bfloat16), scaled_up, (0,), (0,)).astype(jnp.bfloat16)
    grad_inputs = (
        (dims(grad_pre_gate, gate_mat, (1,), (1,)) + dims(grad_pre_up, up_mat, (1,), (1,)))
        .astype(jnp.bfloat16)
        .reshape(slots, chunks, lanes)
    )
    return (grad_gate_mat, grad_up_mat, grad_down_mat, grad_inputs, route_grad)


def local(
    hidden_in, norm_gain, router_weight, grad_out, expert_ids, gate_weight, up_weight, down_weight
):
    f32, bf16 = jnp.float32, jnp.bfloat16
    tok_rows, model_width = hidden_in.shape
    top_count = expert_ids.shape[1]
    experts = router_weight.shape[1]
    capacity = max(2, (tok_rows * top_count * 9 + 8 * experts - 1) // (8 * experts))
    slots = experts * capacity
    lanes = 128
    chunks = model_width // lanes
    axes = ("dp", "expert")

    values = hidden_in.astype(f32)
    inv_rms = lax.rsqrt(jnp.mean(values * values, axis=1, keepdims=True) + 1e-06)
    normed = (values * inv_rms * norm_gain).astype(bf16)
    logits = jnp.dot(normed, router_weight, preferred_element_type=f32)
    chosen = expert_ids[:, :, None] == jnp.arange(experts, dtype=jnp.int32)[None, None, :]
    picked = jnp.sum(jnp.where(chosen, logits[:, None, :], 0.0), axis=2)
    route_prob = jax.nn.softmax(picked, axis=1)
    prob_bf = route_prob.astype(bf16)

    flat_ids = expert_ids.reshape(-1)
    onehot = (flat_ids[:, None] == jnp.arange(experts, dtype=jnp.int32)[None, :]).astype(jnp.int32)
    counts = jnp.cumsum(onehot, axis=0)
    slot_idx = jnp.sum(counts * onehot, axis=1) - 1
    target = (flat_ids * capacity + slot_idx).reshape(tok_rows, top_count)
    slot_te = jnp.sum(jnp.where(chosen, (slot_idx.reshape(tok_rows, top_count) + 1)[:, :, None], 0), axis=1) - 1
    prob_te = jnp.sum(jnp.where(chosen, prob_bf.astype(f32)[:, :, None], 0.0), axis=1)
    sel = slot_te.T[:, None, :] == jnp.arange(capacity, dtype=jnp.int32)[None, :, None]
    sel_tok = sel.reshape(slots, tok_rows).astype(bf16)
    send_p = jnp.sum(jnp.where(sel, prob_te.T[:, None, :], 0.0), axis=2).reshape(slots).astype(bf16)

    send_x = dims(sel_tok, normed, (1,), (0,)).astype(bf16).reshape(experts, capacity, chunks, lanes)
    send_y = dims(sel_tok, grad_out, (1,), (0,)).astype(bf16).reshape(experts, capacity, chunks, lanes)
    recv_x = lax.all_to_all(send_x, axes, 0, 0, tiled=True)
    recv_y = lax.all_to_all(send_y, axes, 0, 0, tiled=True)
    recv_p = lax.all_to_all(send_p.reshape(experts, capacity), axes, 0, 0, tiled=True)

    grad_gate_mat, grad_up_mat, grad_down_mat, grad_inputs, route_grad = expert_backward(
        recv_x.reshape(slots, chunks, lanes),
        recv_y.reshape(slots, chunks, lanes),
        recv_p.reshape(slots),
        gate_weight[0],
        up_weight[0],
        down_weight[0],
    )
    back_inputs = lax.all_to_all(
        grad_inputs.reshape(experts, capacity, chunks, lanes), axes, 0, 0, tiled=True
    )
    back_grads = lax.all_to_all(route_grad.reshape(experts, capacity), axes, 0, 0, tiled=True)

    route_sum = dims(sel_tok, back_inputs.reshape(slots, model_width), (0,), (0,))
    grad_prob = back_grads.reshape(slots)[target].astype(f32)
    grad_picked = route_prob * (grad_prob - jnp.sum(route_prob * grad_prob, axis=1, keepdims=True))
    grad_logit = jnp.sum(jnp.where(chosen, grad_picked[:, :, None], 0.0), axis=1).astype(bf16)
    router_part = dims(normed, grad_logit, (0,), (0,))
    grad_normed = route_sum + dims(grad_logit, router_weight, (1,), (1,))
    gain_part = jnp.sum(grad_normed * values * inv_rms, axis=0)
    n_dev = experts
    rows_per = model_width // n_dev
    gain_per = model_width // n_dev
    gain_rows = jnp.pad(gain_part.reshape(n_dev, 1, gain_per), ((0, 0), (0, 0), (0, experts - gain_per)))
    send_sum = jnp.concatenate([router_part.reshape(n_dev, rows_per, experts), gain_rows], axis=1)
    part_sum = jnp.sum(
        lax.all_to_all(send_sum.astype(bf16), axes, 0, 0, tiled=True).astype(f32), axis=0
    )
    whole = lax.all_to_all(
        jnp.broadcast_to(part_sum.astype(bf16)[None], (n_dev,) + part_sum.shape),
        axes,
        0,
        0,
        tiled=True,
    ).astype(f32)
    grad_router = whole[:, :rows_per, :].reshape(model_width, experts)
    grad_gain = whole[:, rows_per, :gain_per].reshape(model_width)
    scaled = norm_gain * grad_normed
    cube = inv_rms * inv_rms * inv_rms
    grad_hidden = (
        grad_out.astype(f32)
        + inv_rms * scaled
        - values * cube * jnp.mean(scaled * values, axis=1, keepdims=True)
    ).astype(bf16)
    return (
        grad_hidden,
        grad_router,
        grad_gain,
        grad_gate_mat[None],
        grad_up_mat[None],
        grad_down_mat[None],
    )


def solution(mesh):
    in_specs = (
        P(("dp", "expert"), None),
        P(),
        P(),
        P(("dp", "expert"), None),
        P(("dp", "expert"), None),
        P(("dp", "expert"), None, None),
        P(("dp", "expert"), None, None),
        P(("dp", "expert"), None, None),
    )
    out_specs = (
        P(("dp", "expert"), None),
        P(),
        P(),
        P(("dp", "expert"), None, None),
        P(("dp", "expert"), None, None),
        P(("dp", "expert"), None, None),
    )
    return jax.shard_map(local, mesh=mesh, in_specs=in_specs, out_specs=out_specs, check_vma=False)
```

```python
import jax
import jax.numpy as jnp
from jax import lax
from jax.sharding import PartitionSpec as P


def silu_parts(value):
    sigmoid_v = jax.nn.sigmoid(value)
    return (value * sigmoid_v, sigmoid_v * (1.0 + value * (1.0 - sigmoid_v)))


def dims(left, right, left_dims, right_dims):
    return lax.dot_general(
        left, right, ((left_dims, right_dims), ((), ())), preferred_element_type=jnp.float32
    )


def expert_backward(rows_x, rows_y, prob_rows, gate_mat, up_mat, down_mat):
    slots, chunks, lanes = rows_x.shape
    rows_x = rows_x.reshape(slots, chunks * lanes)
    rows_y = rows_y.reshape(slots, chunks * lanes)
    pre_gate = jnp.dot(rows_x, gate_mat, preferred_element_type=jnp.float32)
    pre_up = jnp.dot(rows_x, up_mat, preferred_element_type=jnp.float32)
    activated, derivative = silu_parts(pre_gate)
    hidden_act = activated * pre_up
    grad_mid = dims(rows_y, down_mat, (1,), (1,))
    route_grad = jnp.sum(grad_mid * hidden_act, axis=1).astype(jnp.bfloat16)
    prob_col = prob_rows.astype(jnp.float32)[:, None]
    scaled = prob_col * grad_mid
    grad_pre_gate = (scaled * pre_up * derivative).astype(jnp.bfloat16)
    grad_pre_up = (scaled * activated).astype(jnp.bfloat16)
    scaled_up = (prob_col * rows_y.astype(jnp.float32)).astype(jnp.bfloat16)
    grad_gate_mat = dims(rows_x, grad_pre_gate, (0,), (0,)).astype(jnp.bfloat16)
    grad_up_mat = dims(rows_x, grad_pre_up, (0,), (0,)).astype(jnp.bfloat16)
    grad_down_mat = dims(hidden_act.astype(jnp.bfloat16), scaled_up, (0,), (0,)).astype(jnp.bfloat16)
    grad_inputs = (
        (dims(grad_pre_gate, gate_mat, (1,), (1,)) + dims(grad_pre_up, up_mat, (1,), (1,)))
        .astype(jnp.bfloat16)
        .reshape(slots, chunks, lanes)
    )
    return (grad_gate_mat, grad_up_mat, grad_down_mat, grad_inputs, route_grad)


def local(
    hidden_in, norm_gain, router_weight, grad_out, expert_ids, gate_weight, up_weight, down_weight
):
    f32, bf16 = jnp.float32, jnp.bfloat16
    tok_rows, model_width = hidden_in.shape
    top_count = expert_ids.shape[1]
    experts = router_weight.shape[1]
    capacity = max(2, (tok_rows * top_count * 9 + 8 * experts - 1) // (8 * experts))
    slots = experts * capacity
    lanes = 128
    chunks = model_width // lanes
    axes = ("dp", "expert")

    values = hidden_in.astype(f32)
    inv_rms = lax.rsqrt(jnp.mean(values * values, axis=1, keepdims=True) + 1e-06)
    normed = (values * inv_rms * norm_gain).astype(bf16)
    logits = jnp.dot(normed, router_weight, preferred_element_type=f32)
    chosen = expert_ids[:, :, None] == jnp.arange(experts, dtype=jnp.int32)[None, None, :]
    picked = jnp.sum(jnp.where(chosen, logits[:, None, :], 0.0), axis=2)
    route_prob = jax.nn.softmax(picked, axis=1)
    prob_bf = route_prob.astype(bf16)

    flat_ids = expert_ids.reshape(-1)
    onehot = (flat_ids[:, None] == jnp.arange(experts, dtype=jnp.int32)[None, :]).astype(jnp.int32)
    counts = jnp.cumsum(onehot, axis=0)
    slot_idx = jnp.sum(counts * onehot, axis=1) - 1
    target = (flat_ids * capacity + slot_idx).reshape(tok_rows, top_count)
    hit = target[None, :, :] == jnp.arange(slots, dtype=jnp.int32)[:, None, None]
    sel_tok = jnp.any(hit, axis=2).astype(bf16)
    send_p = jnp.sum(jnp.where(hit, prob_bf.astype(f32)[None], 0.0), axis=(1, 2)).astype(bf16)

    send_x = dims(sel_tok, normed, (1,), (0,)).astype(bf16).reshape(experts, capacity, chunks, lanes)
    send_y = dims(sel_tok, grad_out, (1,), (0,)).astype(bf16).reshape(experts, capacity, chunks, lanes)
    recv_x = lax.all_to_all(send_x, axes, 0, 0, tiled=True)
    recv_x, send_p = lax.optimization_barrier((recv_x, send_p))
    recv_y = lax.all_to_all(send_y, axes, 0, 0, tiled=True)
    recv_p = lax.all_to_all(send_p.reshape(experts, capacity), axes, 0, 0, tiled=True)

    grad_gate_mat, grad_up_mat, grad_down_mat, grad_inputs, route_grad = expert_backward(
        recv_x.reshape(slots, chunks, lanes),
        recv_y.reshape(slots, chunks, lanes),
        recv_p.reshape(slots),
        gate_weight[0],
        up_weight[0],
        down_weight[0],
    )
    back_inputs = lax.all_to_all(
        grad_inputs.reshape(experts, capacity, chunks, lanes), axes, 0, 0, tiled=True
    )
    back_grads = lax.all_to_all(route_grad.reshape(experts, capacity), axes, 0, 0, tiled=True)

    route_sum = dims(sel_tok, back_inputs.reshape(slots, model_width), (0,), (0,))
    grad_prob = back_grads.reshape(slots)[target].astype(f32)
    grad_picked = route_prob * (grad_prob - jnp.sum(route_prob * grad_prob, axis=1, keepdims=True))
    grad_logit = jnp.sum(jnp.where(chosen, grad_picked[:, :, None], 0.0), axis=1).astype(bf16)
    router_part = dims(normed, grad_logit, (0,), (0,))
    grad_normed = route_sum + dims(grad_logit, router_weight, (1,), (1,))
    gain_part = jnp.sum(grad_normed * values * inv_rms, axis=0)
    n_dev = experts
    rows_per = model_width // n_dev
    gain_per = model_width // n_dev
    gain_rows = jnp.pad(gain_part.reshape(n_dev, 1, gain_per), ((0, 0), (0, 0), (0, experts - gain_per)))
    send_sum = jnp.concatenate([router_part.reshape(n_dev, rows_per, experts), gain_rows], axis=1)
    part_sum = jnp.sum(
        lax.all_to_all(send_sum.astype(bf16), axes, 0, 0, tiled=True).astype(f32), axis=0
    )
    whole = lax.all_to_all(
        jnp.broadcast_to(part_sum.astype(bf16)[None], (n_dev,) + part_sum.shape),
        axes,
        0,
        0,
        tiled=True,
    ).astype(f32)
    grad_router = whole[:, :rows_per, :].reshape(model_width, experts)
    grad_gain = whole[:, rows_per, :gain_per].reshape(model_width)
    scaled = norm_gain * grad_normed
    cube = inv_rms * inv_rms * inv_rms
    grad_hidden = (
        grad_out.astype(f32)
        + inv_rms * scaled
        - values * cube * jnp.mean(scaled * values, axis=1, keepdims=True)
    ).astype(bf16)
    return (
        grad_hidden,
        grad_router,
        grad_gain,
        grad_gate_mat[None],
        grad_up_mat[None],
        grad_down_mat[None],
    )


def solution(mesh):
    in_specs = (
        P(("dp", "expert"), None),
        P(),
        P(),
        P(("dp", "expert"), None),
        P(("dp", "expert"), None),
        P(("dp", "expert"), None, None),
        P(("dp", "expert"), None, None),
        P(("dp", "expert"), None, None),
    )
    out_specs = (
        P(("dp", "expert"), None),
        P(),
        P(),
        P(("dp", "expert"), None, None),
        P(("dp", "expert"), None, None),
        P(("dp", "expert"), None, None),
    )
    return jax.shard_map(local, mesh=mesh, in_specs=in_specs, out_specs=out_specs, check_vma=False)
```

```python
import jax
import jax.numpy as jnp
from jax import lax
from jax.sharding import PartitionSpec as P


def silu_parts(value):
    sigmoid_v = jax.nn.sigmoid(value)
    return (value * sigmoid_v, sigmoid_v * (1.0 + value * (1.0 - sigmoid_v)))


def dims(left, right, left_dims, right_dims):
    return lax.dot_general(
        left, right, ((left_dims, right_dims), ((), ())), preferred_element_type=jnp.float32
    )


def expert_backward(rows_x, rows_y, prob_rows, gate_mat, up_mat, down_mat):
    slots, chunks, lanes = rows_x.shape
    rows_x = rows_x.reshape(slots, chunks * lanes)
    rows_y = rows_y.reshape(slots, chunks * lanes)
    pre_gate = jnp.dot(rows_x, gate_mat, preferred_element_type=jnp.float32)
    pre_up = jnp.dot(rows_x, up_mat, preferred_element_type=jnp.float32)
    activated, derivative = silu_parts(pre_gate)
    hidden_act = activated * pre_up
    grad_mid = dims(rows_y, down_mat, (1,), (1,))
    route_grad = jnp.sum(grad_mid * hidden_act, axis=1).astype(jnp.bfloat16)
    prob_col = prob_rows.astype(jnp.float32)[:, None]
    scaled = prob_col * grad_mid
    grad_pre_gate = (scaled * pre_up * derivative).astype(jnp.bfloat16)
    grad_pre_up = (scaled * activated).astype(jnp.bfloat16)
    scaled_up = (prob_col * rows_y.astype(jnp.float32)).astype(jnp.bfloat16)
    grad_gate_mat = dims(rows_x, grad_pre_gate, (0,), (0,)).astype(jnp.bfloat16)
    grad_up_mat = dims(rows_x, grad_pre_up, (0,), (0,)).astype(jnp.bfloat16)
    grad_down_mat = dims(hidden_act.astype(jnp.bfloat16), scaled_up, (0,), (0,)).astype(jnp.bfloat16)
    grad_inputs = (
        (dims(grad_pre_gate, gate_mat, (1,), (1,)) + dims(grad_pre_up, up_mat, (1,), (1,)))
        .astype(jnp.bfloat16)
        .reshape(slots, chunks, lanes)
    )
    return (grad_gate_mat, grad_up_mat, grad_down_mat, grad_inputs, route_grad)


def local(
    hidden_in, norm_gain, router_weight, grad_out, expert_ids, gate_weight, up_weight, down_weight
):
    f32, bf16 = jnp.float32, jnp.bfloat16
    tok_rows, model_width = hidden_in.shape
    top_count = expert_ids.shape[1]
    experts = router_weight.shape[1]
    capacity = max(2, (tok_rows * top_count * 9 + 8 * experts - 1) // (8 * experts))
    slots = experts * capacity
    lanes = 128
    chunks = model_width // lanes
    axes = ("dp", "expert")

    values = hidden_in.astype(f32)
    inv_rms = lax.rsqrt(jnp.mean(values * values, axis=1, keepdims=True) + 1e-06)
    normed = (values * inv_rms * norm_gain).astype(bf16)
    logits = jnp.dot(normed, router_weight, preferred_element_type=f32)
    chosen = expert_ids[:, :, None] == jnp.arange(experts, dtype=jnp.int32)[None, None, :]
    picked = jnp.sum(jnp.where(chosen, logits[:, None, :], 0.0), axis=2)
    route_prob = jax.nn.softmax(picked, axis=1)
    prob_bf = route_prob.astype(bf16)

    flat_ids = expert_ids.reshape(-1)
    onehot = (flat_ids[:, None] == jnp.arange(experts, dtype=jnp.int32)[None, :]).astype(jnp.int32)
    counts = jnp.cumsum(onehot, axis=0)
    slot_idx = jnp.sum(counts * onehot, axis=1) - 1
    target = (flat_ids * capacity + slot_idx).reshape(tok_rows, top_count)
    hit = target[None, :, :] == jnp.arange(slots, dtype=jnp.int32)[:, None, None]
    sel_tok = jnp.any(hit, axis=2).astype(bf16)
    send_p = jnp.sum(jnp.where(hit, prob_bf.astype(f32)[None], 0.0), axis=(1, 2)).astype(bf16)

    send_x = dims(sel_tok, normed, (1,), (0,)).astype(bf16).reshape(experts, capacity, chunks, lanes)
    send_y = dims(sel_tok, grad_out, (1,), (0,)).astype(bf16).reshape(experts, capacity, chunks, lanes)
    recv_x = lax.all_to_all(send_x, axes, 0, 0, tiled=True)
    recv_x, send_p = lax.optimization_barrier((recv_x, send_p))
    recv_y = lax.all_to_all(send_y, axes, 0, 0, tiled=True)
    recv_p = lax.all_to_all(send_p.reshape(experts, capacity), axes, 0, 0, tiled=True)

    grad_gate_mat, grad_up_mat, grad_down_mat, grad_inputs, route_grad = expert_backward(
        recv_x.reshape(slots, chunks, lanes),
        recv_y.reshape(slots, chunks, lanes),
        recv_p.reshape(slots),
        gate_weight[0],
        up_weight[0],
        down_weight[0],
    )
    back_inputs = lax.all_to_all(
        grad_inputs.reshape(experts, capacity, chunks, lanes), axes, 0, 0, tiled=True
    )
    back_inputs, route_grad = lax.optimization_barrier((back_inputs, route_grad))
    back_grads = lax.all_to_all(route_grad.reshape(experts, capacity), axes, 0, 0, tiled=True)

    route_sum = dims(sel_tok, back_inputs.reshape(slots, model_width), (0,), (0,))
    grad_prob = back_grads.reshape(slots)[target].astype(f32)
    grad_picked = route_prob * (grad_prob - jnp.sum(route_prob * grad_prob, axis=1, keepdims=True))
    grad_logit = jnp.sum(jnp.where(chosen, grad_picked[:, :, None], 0.0), axis=1).astype(bf16)
    router_part = dims(normed, grad_logit, (0,), (0,))
    grad_normed = route_sum + dims(grad_logit, router_weight, (1,), (1,))
    gain_part = jnp.sum(grad_normed * values * inv_rms, axis=0)
    n_dev = experts
    rows_per = model_width // n_dev
    gain_per = model_width // n_dev
    gain_rows = jnp.pad(gain_part.reshape(n_dev, 1, gain_per), ((0, 0), (0, 0), (0, experts - gain_per)))
    send_sum = jnp.concatenate([router_part.reshape(n_dev, rows_per, experts), gain_rows], axis=1)
    part_sum = jnp.sum(
        lax.all_to_all(send_sum.astype(bf16), axes, 0, 0, tiled=True).astype(f32), axis=0
    )
    whole = lax.all_to_all(
        jnp.broadcast_to(part_sum.astype(bf16)[None], (n_dev,) + part_sum.shape),
        axes,
        0,
        0,
        tiled=True,
    ).astype(f32)
    grad_router = whole[:, :rows_per, :].reshape(model_width, experts)
    grad_gain = whole[:, rows_per, :gain_per].reshape(model_width)
    scaled = norm_gain * grad_normed
    cube = inv_rms * inv_rms * inv_rms
    grad_hidden = (
        grad_out.astype(f32)
        + inv_rms * scaled
        - values * cube * jnp.mean(scaled * values, axis=1, keepdims=True)
    ).astype(bf16)
    return (
        grad_hidden,
        grad_router,
        grad_gain,
        grad_gate_mat[None],
        grad_up_mat[None],
        grad_down_mat[None],
    )


def solution(mesh):
    in_specs = (
        P(("dp", "expert"), None),
        P(),
        P(),
        P(("dp", "expert"), None),
        P(("dp", "expert"), None),
        P(("dp", "expert"), None, None),
        P(("dp", "expert"), None, None),
        P(("dp", "expert"), None, None),
    )
    out_specs = (
        P(("dp", "expert"), None),
        P(),
        P(),
        P(("dp", "expert"), None, None),
        P(("dp", "expert"), None, None),
        P(("dp", "expert"), None, None),
    )
    return jax.shard_map(local, mesh=mesh, in_specs=in_specs, out_specs=out_specs, check_vma=False)
```
